128 devices in a mesh: grp: 4 (over x), gx: 4 (over y), gy: 8 (over z, core).
Axes of the slice: x: 4, y: 4, z: 4, core: 2. Of those that a mesh axis runs over, the one named last changes fastest.
Arguments:
- modes_now: float32 [4, 32, 512, 1024], P('grp', ('gx', 'gy')), may hold values from -6 to 6
- modes_old: float32 [4, 32, 512, 1024], P('grp', ('gx', 'gy')), may hold values from -6 to 6
- pressure_now: float32 [4, 32, 512, 1024], P('grp', None, 'gx', 'gy'), may hold values from -6 to 6
- source: float32 [4, 32, 512, 1024], P('grp', None, 'gx', 'gy'), may hold values from -6 to 6
- strip_slot: int32 [4, 512, 8], P('grp', 'gx', 'gy'), may hold values from 0 to 255, as said below
- strip_row: int32 [4, 512, 8], P('grp', 'gx', 'gy'), may hold values from 0 to 127, as said below
Outputs:
- modes_new: float32 [4, 32, 512, 1024], P('grp', ('gx', 'gy'))
- pressure_next: float32 [4, 32, 512, 1024], P('grp', None, 'gx', 'gy')
The draws below stay inside these ranges and needn't reach their ends.
Inputs may be any that keep to these rules, and one draw needn't show every extreme that they name: The 128 strips of one device take distinct values of strip_slot. Each device sends to every other device (itself included) either no strip or exactly 2, and every bottom-face strip of every device is met by exactly one top-face strip. `strip_row`: see strip_slot.
All inputs are finite; a program needn't handle non-finite values.
Results may differ from the reference program's by a relative error of at most 0.00007.
Values sent between devices are 32-bit elements; how exact they have to be, the bound alone decides.
No kernel may reach another device: no remote copies, remote signals or barrier semaphores. Data moves between devices by JAX's collectives and lax.ppermute only.
A program may use at most 64 MiB of HBM per device.

```python
import jax
import jax.numpy as jnp
from jax import lax

NXR = 512
NYR = 1024
NZ = 32
RECTS = 4
CX = 128
CY = 128
CAP = 2
N_GRP = 4
N_GX = 4
N_GY = 8
DEVICES = 128


def strip_plan(key):
    count = DEVICES
    per = CX
    slots_per = CAP
    groups = per // slots_per
    values = jnp.arange(count, dtype=jnp.int32)
    ranks = jax.random.permutation(jax.random.fold_in(key, 11), count).astype(jnp.int32)
    scores = jnp.where(values == count // 2, -2, jnp.where(values == count - 1, -1, ranks))
    offsets = jnp.argsort(scores, stable=True).astype(jnp.int32)[:groups]
    keys_send = jax.random.split(jax.random.fold_in(key, 12), count)
    order = jax.vmap(lambda one: jax.random.permutation(one, per))(keys_send).astype(jnp.int32)
    keys_recv = jax.random.split(jax.random.fold_in(key, 13), count)
    placing = jax.vmap(lambda one: jax.random.permutation(one, per))(keys_recv).astype(jnp.int32)
    sender = jnp.arange(count, dtype=jnp.int32)[:, None]
    position = jnp.arange(per, dtype=jnp.int32)[None, :]
    partner = (sender + offsets[position // slots_per]) % count
    slot_value = partner * slots_per + position % slots_per
    row_value = placing[partner, jnp.broadcast_to(position, partner.shape)]
    sender_full = jnp.broadcast_to(sender, partner.shape)
    slot_table = jnp.zeros((count, per), jnp.int32).at[sender_full, order].set(slot_value)
    row_table = jnp.zeros((count, per), jnp.int32).at[sender_full, order].set(row_value)
    return (slot_table, row_table)


def arrange(table):
    return table.reshape(N_GRP, N_GX, N_GY, CX).transpose(0, 1, 3, 2).reshape(N_GRP, NXR, N_GY)


def draw_strip_slot(key, part):
    slot_table, row_table = strip_plan(jax.random.fold_in(key, 5))
    return arrange(slot_table)


def draw_strip_row(key, part):
    slot_table, row_table = strip_plan(jax.random.fold_in(key, 5))
    return arrange(row_table)


def block_levels(stream_key, shape, pieces, low, high):
    def one(dim, blocks):
        draws = jax.random.uniform(jax.random.fold_in(jax.random.fold_in(stream_key, 6), dim), (blocks,), jnp.float32, low / len(pieces), high / len(pieces))
        return jnp.repeat(jnp.exp(draws), shape[dim] // blocks).reshape((-1,) + (1,) * (len(shape) - dim - 1))

    loudness = one(*pieces[0])
    for cut in pieces[1:]:
        loudness = loudness * one(*cut)
    return loudness


def scatter_about(stream_key, shape, width, reach, cuts=(), kind=jnp.bfloat16):
    result = width * jax.random.normal(stream_key, shape, jnp.float32)
    if cuts:
        result = result * block_levels(stream_key, shape, cuts, -0.22, 0.18)
    return jnp.clip(result, -reach, reach).astype(kind)


def setup_inputs(seed: int = 0) -> dict:
    key_list = jax.random.split(jax.random.key(seed), 7)
    return {
        "modes_now": scatter_about(key_list[0], (RECTS, NZ, NXR, NYR), 1.0, 6.0, ((0, 4), (1, 32)), jnp.float32),
        "modes_old": scatter_about(key_list[1], (RECTS, NZ, NXR, NYR), 1.0, 6.0, ((0, 4), (1, 32)), jnp.float32),
        "pressure_now": scatter_about(key_list[2], (RECTS, NZ, NXR, NYR), 1.0, 6.0, ((0, 4), (2, 4), (3, 8)), jnp.float32),
        "source": scatter_about(key_list[3], (RECTS, NZ, NXR, NYR), 1.0, 6.0, ((0, 4), (2, 4), (3, 8)), jnp.float32),
        "strip_slot": draw_strip_slot(jax.random.fold_in(key_list[6], 71), 0),
        "strip_row": draw_strip_row(jax.random.fold_in(key_list[6], 71), 0),
    }


COURANT = 0.5
WEIGHTS = (1.5, -0.15, 2.0 / 180.0)
HIGH = lax.Precision.HIGHEST

def cosine_table(count):
    rows = jnp.arange(count, dtype=jnp.int32).astype(jnp.float32)[:, None]
    cols = jnp.arange(count, dtype=jnp.int32).astype(jnp.float32)[None, :]
    scale = jnp.where(rows == 0, jnp.sqrt(1.0 / count), jnp.sqrt(2.0 / count))
    return (scale * jnp.cos(jnp.pi * rows * (cols + 0.5) / count)).astype(jnp.float32)

def face_stencil(diff):
    first = diff[..., 0, :]
    second = diff[..., 1, :]
    third = diff[..., 2, :]
    return jnp.stack([WEIGHTS[0] * first + WEIGHTS[1] * second + WEIGHTS[2] * third, WEIGHTS[1] * first + WEIGHTS[2] * second, WEIGHTS[2] * first], axis=-2)

def advance(current, previous, spectrum, depth_index, depth, long_x, long_y):
    index_x = jnp.arange(long_x, dtype=jnp.int32).astype(jnp.float32)
    index_y = jnp.arange(long_y, dtype=jnp.int32).astype(jnp.float32)
    part_z = depth_index / depth * (depth_index / depth)
    part_x = index_x / long_x * (index_x / long_x)
    part_y = index_y / long_y * (index_y / long_y)
    theta = COURANT * jnp.pi * jnp.sqrt(part_z[:, None, None] + part_x[None, :, None] + part_y[None, None, :])
    shape = jnp.sinc(theta / (2.0 * jnp.pi))
    return 2.0 * jnp.cos(theta) * current - previous + COURANT * COURANT * shape * shape * spectrum

def forward_field(field, table_z, table_x, table_y):
    part = jnp.einsum('kz,zxy->kxy', table_z, field, precision=HIGH)
    part = jnp.einsum('bx,kxy->kby', table_x, part, precision=HIGH)
    return jnp.einsum('cy,kby->kbc', table_y, part, precision=HIGH)

def inverse_field(modes, table_z, table_x, table_y):
    part = jnp.einsum('cy,abc->aby', table_y, modes, precision=HIGH)
    part = jnp.einsum('bx,aby->axy', table_x, part, precision=HIGH)
    return jnp.einsum('az,axy->zxy', table_z, part, precision=HIGH)

def to_strips(layers):
    return layers.reshape(RECTS, 3, NXR, N_GY, CY).transpose(0, 2, 3, 1, 4)

def from_strips(strips):
    return strips.transpose(0, 3, 1, 2, 4).reshape(RECTS, 3, NXR, NYR)

def reference(modes_now, modes_old, pressure_now, source, strip_slot, strip_row):
    table_z = cosine_table(NZ)
    table_x = cosine_table(NXR)
    table_y = cosine_table(NYR)
    pressure = pressure_now
    top_layers = jnp.stack([pressure[:, NZ - 1], pressure[:, NZ - 2], pressure[:, NZ - 3]], axis=1)
    top_strips = to_strips(top_layers)
    bottom_strips = to_strips(pressure[:, 0:3])
    partner = strip_slot // CAP
    group_p = partner // (N_GX * N_GY)
    block_x = partner // N_GY % N_GX
    block_y = partner % N_GY
    row_p = block_x * CX + strip_row
    met = bottom_strips[group_p, row_p, block_y]
    force = face_stencil(met - top_strips)
    bottom_force = jnp.zeros_like(bottom_strips).at[group_p, row_p, block_y].add(-force)
    bottom_field = from_strips(bottom_force)
    top_field = from_strips(force)
    forcing = source.at[:, 0:3].add(bottom_field)
    forcing = forcing.at[:, NZ - 1].add(top_field[:, 0])
    forcing = forcing.at[:, NZ - 2].add(top_field[:, 1])
    forcing = forcing.at[:, NZ - 3].add(top_field[:, 2])
    depth_index = jnp.arange(NZ, dtype=jnp.int32).astype(jnp.float32)

    def step_one(items):
        field, current, previous = items
        spectrum = forward_field(field, table_z, table_x, table_y)
        return advance(current, previous, spectrum, depth_index, NZ, NXR, NYR)
    modes_new = lax.map(step_one, (forcing, modes_now, modes_old))
    pressure_next = lax.map(lambda one: inverse_field(one, table_z, table_x, table_y), modes_new)
    return (modes_new, pressure_next)
```

```python
import jax
import jax.numpy as jnp
from jax import lax
from jax.sharding import PartitionSpec as P

COURANT = 0.5
WEIGHTS = (1.5, -0.15, 2.0 / 180.0)
HIGH = lax.Precision.HIGHEST
FAST = lax.Precision.HIGH


def cosine_table(count):
    rows = jnp.arange(count, dtype=jnp.int32).astype(jnp.float32)[:, None]
    cols = jnp.arange(count, dtype=jnp.int32).astype(jnp.float32)[None, :]
    scale = jnp.where(rows == 0, jnp.sqrt(1.0 / count), jnp.sqrt(2.0 / count))
    return scale * jnp.cos(jnp.pi * rows * (cols + 0.5) / count)


def face_stencil(diff):
    first = diff[..., 0, :]
    second = diff[..., 1, :]
    third = diff[..., 2, :]
    return jnp.stack(
        [
            WEIGHTS[0] * first + WEIGHTS[1] * second + WEIGHTS[2] * third,
            WEIGHTS[1] * first + WEIGHTS[2] * second,
            WEIGHTS[2] * first,
        ],
        axis=-2,
    )


def advance(current, previous, spectrum, depth_index, depth, long_x, long_y):
    index_x = jnp.arange(long_x, dtype=jnp.int32).astype(jnp.float32)
    index_y = jnp.arange(long_y, dtype=jnp.int32).astype(jnp.float32)
    part_z = depth_index / depth * (depth_index / depth)
    part_x = index_x / long_x * (index_x / long_x)
    part_y = index_y / long_y * (index_y / long_y)
    theta = (
        COURANT
        * jnp.pi
        * jnp.sqrt(part_z[:, None, None] + part_x[None, :, None] + part_y[None, None, :])
    )
    shape = jnp.sinc(theta / (2.0 * jnp.pi))
    return 2.0 * jnp.cos(theta) * current - previous + COURANT * COURANT * shape * shape * spectrum


def to_modes(field, table_z, table_x, table_y):
    width_x = lax.axis_size("gx")
    width_y = lax.axis_size("gy")
    rows_x = field.shape[2]
    cols_y = field.shape[3]
    part = jnp.einsum("kz,zxy->kxy", table_z, field[0], precision=HIGH)
    part = lax.all_to_all(part, ("gx", "gy"), split_axis=0, concat_axis=0, tiled=True)
    part = part.reshape(width_x, width_y, rows_x, cols_y)
    split_x = table_x.reshape(table_x.shape[0], width_x, rows_x)
    split_y = table_y.reshape(table_y.shape[0], width_y, cols_y)
    part = jnp.einsum("bix,ijxy->bjy", split_x, part, precision=FAST)
    return jnp.einsum("cjy,bjy->bc", split_y, part, precision=FAST)[None, None]


def to_cells(modes, table_z, table_x, table_y):
    width_x = lax.axis_size("gx")
    width_y = lax.axis_size("gy")
    rows_x = modes.shape[2] // width_x
    cols_y = modes.shape[3] // width_y
    split_x = table_x.reshape(table_x.shape[0], width_x, rows_x)
    split_y = table_y.reshape(table_y.shape[0], width_y, cols_y)
    part = jnp.einsum("cjy,bc->bjy", split_y, modes[0, 0], precision=FAST)
    part = jnp.einsum("bix,bjy->ijxy", split_x, part, precision=FAST)
    part = part.reshape(width_x * width_y, rows_x, cols_y)
    cells = lax.all_to_all(part, ("gx", "gy"), split_axis=0, concat_axis=0, tiled=True)
    return jnp.einsum("kz,kxy->zxy", table_z, cells, precision=HIGH)[None]


def strip_terms(rims, marks, bottom):
    live = marks >= 0
    safe = jnp.where(live, marks, 0)
    met = bottom[safe]
    force = face_stencil(met - rims) * live[..., None, None].astype(jnp.float32)
    return (force, safe)


def shards(modes_now, modes_old, pressure_now, source, strip_slot, strip_row):
    depth = source.shape[1]
    rows_x = source.shape[2]
    cols_y = source.shape[3]
    planes = modes_now.shape[1]
    long_x = modes_now.shape[2]
    long_y = modes_now.shape[3]
    table_z = cosine_table(depth)
    table_x = cosine_table(long_x)
    table_y = cosine_table(long_y)
    top = jnp.stack(
        [pressure_now[0, depth - 1], pressure_now[0, depth - 2], pressure_now[0, depth - 3]], axis=1
    )
    bottom = jnp.transpose(pressure_now[0, 0:3], (1, 0, 2))
    devices = lax.axis_size(("grp", "gx", "gy"))
    slots_per = max(2, rows_x // devices)
    slots = strip_slot.reshape(-1)
    rows = strip_row.reshape(-1)
    buffer = jnp.zeros((devices * slots_per, 3, cols_y), jnp.float32).at[slots].set(top)
    labels = jnp.full((devices * slots_per,), -1, jnp.int32).at[slots].set(rows)
    rims = lax.all_to_all(
        buffer.reshape(devices, slots_per, 3, cols_y),
        ("grp", "gx", "gy"),
        split_axis=0,
        concat_axis=0,
        tiled=True,
    )
    marks = lax.all_to_all(
        labels.reshape(devices, slots_per),
        ("grp", "gx", "gy"),
        split_axis=0,
        concat_axis=0,
        tiled=True,
    )
    force, safe = strip_terms(rims, marks, bottom)
    back = lax.all_to_all(force, ("grp", "gx", "gy"), split_axis=0, concat_axis=0, tiled=True)
    back, force, safe = (back, force, safe)
    top_force = back.reshape(-1, 3, cols_y)[slots]
    bottom_force = (
        jnp.zeros((rows_x, 3, cols_y), jnp.float32)
        .at[safe.reshape(-1)]
        .add(-force.reshape(-1, 3, cols_y))
    )
    forcing = source.at[:, 0:3].add(jnp.transpose(bottom_force, (1, 0, 2))[None])
    forcing = forcing.at[:, depth - 1].add(top_force[:, 0][None])
    forcing = forcing.at[:, depth - 2].add(top_force[:, 1][None])
    forcing = forcing.at[:, depth - 3].add(top_force[:, 2][None])
    spectrum = to_modes(forcing, table_z, table_x, table_y)
    block = lax.axis_index(("gx", "gy"))
    depth_index = (block * planes + jnp.arange(planes, dtype=jnp.int32)).astype(jnp.float32)
    modes_new = advance(
        modes_now[0], modes_old[0], spectrum[0], depth_index, depth, long_x, long_y
    )[None]
    pressure_next = to_cells(modes_new, table_z, table_x, table_y)
    return (modes_new, pressure_next)


def solution(mesh):
    placed = (
        P("grp", ("gx", "gy"), None, None),
        P("grp", ("gx", "gy"), None, None),
        P("grp", None, "gx", "gy"),
        P("grp", None, "gx", "gy"),
        P("grp", "gx", "gy"),
        P("grp", "gx", "gy"),
    )
    return jax.shard_map(
        shards,
        mesh=mesh,
        in_specs=placed,
        out_specs=(P("grp", ("gx", "gy"), None, None), P("grp", None, "gx", "gy")),
        check_vma=False,
    )
```

```python
import jax
import jax.numpy as jnp
from jax import lax
from jax.sharding import PartitionSpec as P

COURANT = 0.5
WEIGHTS = (1.5, -0.15, 2.0 / 180.0)
HIGH = lax.Precision.HIGHEST
FAST = lax.Precision.HIGH


def cosine_table(count):
    rows = jnp.arange(count, dtype=jnp.int32).astype(jnp.float32)[:, None]
    cols = jnp.arange(count, dtype=jnp.int32).astype(jnp.float32)[None, :]
    scale = jnp.where(rows == 0, jnp.sqrt(1.0 / count), jnp.sqrt(2.0 / count))
    return scale * jnp.cos(jnp.pi * rows * (cols + 0.5) / count)


def face_stencil(diff):
    first = diff[..., 0, :]
    second = diff[..., 1, :]
    third = diff[..., 2, :]
    return jnp.stack(
        [
            WEIGHTS[0] * first + WEIGHTS[1] * second + WEIGHTS[2] * third,
            WEIGHTS[1] * first + WEIGHTS[2] * second,
            WEIGHTS[2] * first,
        ],
        axis=-2,
    )


def to_modes(field, table_z, table_x, table_y):
    width_x = lax.axis_size("gx")
    width_y = lax.axis_size("gy")
    rows_x = field.shape[2]
    cols_y = field.shape[3]
    part = jnp.einsum("kz,zxy->kxy", table_z, field[0], precision=HIGH)
    part = lax.all_to_all(part, ("gx", "gy"), split_axis=0, concat_axis=0, tiled=True)
    part = part.reshape(width_x, width_y, rows_x, cols_y)
    split_x = table_x.reshape(table_x.shape[0], width_x, rows_x)
    split_y = table_y.reshape(table_y.shape[0], width_y, cols_y)
    part = jnp.einsum("bix,ijxy->bjy", split_x, part, precision=FAST)
    return jnp.einsum("cjy,bjy->bc", split_y, part, precision=FAST)[None, None]


def to_cells(modes, table_z, table_x, table_y):
    width_x = lax.axis_size("gx")
    width_y = lax.axis_size("gy")
    rows_x = modes.shape[2] // width_x
    cols_y = modes.shape[3] // width_y
    split_x = table_x.reshape(table_x.shape[0], width_x, rows_x)
    split_y = table_y.reshape(table_y.shape[0], width_y, cols_y)
    part = jnp.einsum("cjy,bc->bjy", split_y, modes[0, 0], precision=FAST)
    part = jnp.einsum("bix,bjy->ijxy", split_x, part, precision=FAST)
    part = part.reshape(width_x * width_y, rows_x, cols_y)
    cells = lax.all_to_all(part, ("gx", "gy"), split_axis=0, concat_axis=0, tiled=True)
    return jnp.einsum("kz,kxy->zxy", table_z, cells, precision=HIGH)[None]


def advance_terms(depth_index, depth, long_x, long_y):
    index_x = jnp.arange(long_x, dtype=jnp.int32).astype(jnp.float32)
    index_y = jnp.arange(long_y, dtype=jnp.int32).astype(jnp.float32)
    part_z = depth_index / depth * (depth_index / depth)
    part_x = index_x / long_x * (index_x / long_x)
    part_y = index_y / long_y * (index_y / long_y)
    theta = (
        COURANT
        * jnp.pi
        * jnp.sqrt(part_z[:, None, None] + part_x[None, :, None] + part_y[None, None, :])
    )
    shape = jnp.sinc(theta / (2.0 * jnp.pi))
    return 2.0 * jnp.cos(theta), COURANT * COURANT * shape * shape


def one_hot(index, count):
    return (index[:, None] == jnp.arange(count, dtype=jnp.int32)[None, :]).astype(jnp.float32)


def shards(modes_now, modes_old, pressure_now, source, strip_slot, strip_row):
    depth = source.shape[1]
    rows_x = source.shape[2]
    cols_y = source.shape[3]
    planes = modes_now.shape[1]
    long_x = modes_now.shape[2]
    long_y = modes_now.shape[3]
    block = lax.axis_index(("gx", "gy"))
    depth_index = (block * planes + jnp.arange(planes, dtype=jnp.int32)).astype(jnp.float32)
    table_z, table_x, table_y, scale_now, scale_spec = lax.optimization_barrier(
        (cosine_table(depth), cosine_table(long_x), cosine_table(long_y))
        + advance_terms(depth_index, depth, long_x, long_y)
    )
    top = jnp.stack(
        [pressure_now[0, depth - 1], pressure_now[0, depth - 2], pressure_now[0, depth - 3]], axis=1
    ).reshape(rows_x, 3 * cols_y)
    bottom = jnp.transpose(pressure_now[0, 0:3], (1, 0, 2)).reshape(rows_x, 3 * cols_y)
    devices = lax.axis_size(("grp", "gx", "gy"))
    slots_per = max(2, rows_x // devices)
    total = devices * slots_per
    slots = strip_slot.reshape(-1)
    rows = strip_row.reshape(-1)
    label = jnp.broadcast_to((rows + 1).astype(jnp.float32)[:, None], (rows_x, cols_y))
    send = one_hot(slots, total)
    payload = jnp.concatenate([top, label], axis=1)
    buffer = jnp.einsum("sk,sf->kf", send, payload, precision=HIGH)
    got = lax.all_to_all(buffer, ("grp", "gx", "gy"), split_axis=0, concat_axis=0, tiled=True)
    rims = got[:, : 3 * cols_y].reshape(total, 3, cols_y)
    marks = jnp.round(got[:, 3 * cols_y]).astype(jnp.int32) - 1
    live = marks >= 0
    meet = one_hot(marks, rows_x)
    met = jnp.einsum("kr,rf->kf", meet, bottom, precision=HIGH).reshape(total, 3, cols_y)
    force = face_stencil(met - rims) * live[:, None, None].astype(jnp.float32)
    force = force.reshape(total, 3 * cols_y)
    back = lax.all_to_all(force, ("grp", "gx", "gy"), split_axis=0, concat_axis=0, tiled=True)
    top_force = jnp.einsum("sk,kf->sf", send, back, precision=HIGH).reshape(rows_x, 3, cols_y)
    bottom_force = jnp.einsum("kr,kf->rf", meet, -force, precision=HIGH).reshape(rows_x, 3, cols_y)
    forcing = source.at[:, 0:3].add(jnp.transpose(bottom_force, (1, 0, 2))[None])
    forcing = forcing.at[:, depth - 1].add(top_force[:, 0][None])
    forcing = forcing.at[:, depth - 2].add(top_force[:, 1][None])
    forcing = forcing.at[:, depth - 3].add(top_force[:, 2][None])
    spectrum = to_modes(forcing, table_z, table_x, table_y)
    modes_new = (scale_now * modes_now[0] - modes_old[0] + scale_spec * spectrum[0])[None]
    pressure_next = to_cells(modes_new, table_z, table_x, table_y)
    return (modes_new, pressure_next)


def solution(mesh):
    placed = (
        P("grp", ("gx", "gy"), None, None),
        P("grp", ("gx", "gy"), None, None),
        P("grp", None, "gx", "gy"),
        P("grp", None, "gx", "gy"),
        P("grp", "gx", "gy"),
        P("grp", "gx", "gy"),
    )
    return jax.shard_map(
        shards,
        mesh=mesh,
        in_specs=placed,
        out_specs=(P("grp", ("gx", "gy"), None, None), P("grp", None, "gx", "gy")),
        check_vma=False,
    )
```

```python
import jax
import jax.numpy as jnp
from jax import lax
from jax.sharding import PartitionSpec as P

COURANT = 0.5
WEIGHTS = (1.5, -0.15, 2.0 / 180.0)
HIGH = lax.Precision.HIGHEST
FAST = lax.Precision.HIGH


def cosine_table(count):
    rows = jnp.arange(count, dtype=jnp.int32).astype(jnp.float32)[:, None]
    cols = jnp.arange(count, dtype=jnp.int32).astype(jnp.float32)[None, :]
    scale = jnp.where(rows == 0, jnp.sqrt(1.0 / count), jnp.sqrt(2.0 / count))
    return scale * jnp.cos(jnp.pi * rows * (cols + 0.5) / count)


def face_stencil(diff):
    first = diff[..., 0, :]
    second = diff[..., 1, :]
    third = diff[..., 2, :]
    return jnp.stack(
        [
            WEIGHTS[0] * first + WEIGHTS[1] * second + WEIGHTS[2] * third,
            WEIGHTS[1] * first + WEIGHTS[2] * second,
            WEIGHTS[2] * first,
        ],
        axis=-2,
    )


def to_modes(field, table_z, table_x, table_y):
    width_x = lax.axis_size("gx")
    width_y = lax.axis_size("gy")
    rows_x = field.shape[2]
    cols_y = field.shape[3]
    part = jnp.einsum("kz,zxy->kxy", table_z, field[0], precision=HIGH)
    part = lax.all_to_all(part, ("gx", "gy"), split_axis=0, concat_axis=0, tiled=True)
    part = part.reshape(width_x, width_y, rows_x, cols_y)
    split_x = table_x.reshape(table_x.shape[0], width_x, rows_x)
    split_y = table_y.reshape(table_y.shape[0], width_y, cols_y)
    part = jnp.einsum("bix,ijxy->bjy", split_x, part, precision=FAST)
    return jnp.einsum("cjy,bjy->bc", split_y, part, precision=FAST)[None, None]


def to_cells(modes, table_z, table_x, table_y):
    width_x = lax.axis_size("gx")
    width_y = lax.axis_size("gy")
    rows_x = modes.shape[2] // width_x
    cols_y = modes.shape[3] // width_y
    split_x = table_x.reshape(table_x.shape[0], width_x, rows_x)
    split_y = table_y.reshape(table_y.shape[0], width_y, cols_y)
    part = jnp.einsum("cjy,bc->bjy", split_y, modes[0, 0], precision=FAST)
    part = jnp.einsum("bix,bjy->ijxy", split_x, part, precision=FAST)
    part = part.reshape(width_x * width_y, rows_x, cols_y)
    cells = lax.all_to_all(part, ("gx", "gy"), split_axis=0, concat_axis=0, tiled=True)
    return jnp.einsum("kz,kxy->zxy", table_z, cells, precision=HIGH)[None]


def advance_terms(depth_index, depth, long_x, long_y):
    index_x = jnp.arange(long_x, dtype=jnp.int32).astype(jnp.float32)
    index_y = jnp.arange(long_y, dtype=jnp.int32).astype(jnp.float32)
    part_z = depth_index / depth * (depth_index / depth)
    part_x = index_x / long_x * (index_x / long_x)
    part_y = index_y / long_y * (index_y / long_y)
    theta = (
        COURANT
        * jnp.pi
        * jnp.sqrt(part_z[:, None, None] + part_x[None, :, None] + part_y[None, None, :])
    )
    shape = jnp.sinc(theta / (2.0 * jnp.pi))
    return 2.0 * jnp.cos(theta), COURANT * COURANT * shape * shape


def one_hot(index, count):
    return (index[:, None] == jnp.arange(count, dtype=jnp.int32)[None, :]).astype(jnp.float32)


def shards(modes_now, modes_old, pressure_now, source, strip_slot, strip_row):
    depth = source.shape[1]
    rows_x = source.shape[2]
    cols_y = source.shape[3]
    planes = modes_now.shape[1]
    long_x = modes_now.shape[2]
    long_y = modes_now.shape[3]
    block = lax.axis_index(("gx", "gy"))
    depth_index = (block * planes + jnp.arange(planes, dtype=jnp.int32)).astype(jnp.float32)
    table_z = lax.optimization_barrier(cosine_table(depth))
    table_x = lax.optimization_barrier(cosine_table(long_x))
    table_y = lax.optimization_barrier(cosine_table(long_y))
    scale_now, scale_spec = advance_terms(depth_index, depth, long_x, long_y)
    scale_now = lax.optimization_barrier(scale_now)
    scale_spec = lax.optimization_barrier(scale_spec)
    top = jnp.stack(
        [pressure_now[0, depth - 1], pressure_now[0, depth - 2], pressure_now[0, depth - 3]], axis=1
    ).reshape(rows_x, 3 * cols_y)
    bottom = jnp.transpose(pressure_now[0, 0:3], (1, 0, 2)).reshape(rows_x, 3 * cols_y)
    devices = lax.axis_size(("grp", "gx", "gy"))
    slots_per = max(2, rows_x // devices)
    total = devices * slots_per
    slots = strip_slot.reshape(-1)
    rows = strip_row.reshape(-1)
    label = jnp.broadcast_to((rows + 1).astype(jnp.float32)[:, None], (rows_x, cols_y))
    send = one_hot(slots, total)
    payload = jnp.concatenate([top, label], axis=1)
    buffer = jnp.einsum("sk,sf->kf", send, payload, precision=HIGH)
    got = lax.all_to_all(buffer, ("grp", "gx", "gy"), split_axis=0, concat_axis=0, tiled=True)
    rims = got[:, : 3 * cols_y]
    marks = jnp.round(got[:, 3 * cols_y]).astype(jnp.int32) - 1
    live = (marks >= 0).astype(jnp.float32)[:, None]
    meet = one_hot(marks, rows_x)
    met = jnp.einsum("kr,rf->kf", meet, bottom, precision=HIGH)
    diff = met - rims
    first = diff[:, :cols_y]
    second = diff[:, cols_y : 2 * cols_y]
    third = diff[:, 2 * cols_y :]
    force = jnp.concatenate(
        [
            WEIGHTS[0] * first + WEIGHTS[1] * second + WEIGHTS[2] * third,
            WEIGHTS[1] * first + WEIGHTS[2] * second,
            WEIGHTS[2] * first,
        ],
        axis=1,
    ) * live
    back = lax.all_to_all(force, ("grp", "gx", "gy"), split_axis=0, concat_axis=0, tiled=True)
    top_force = jnp.einsum("sk,kf->sf", send, back, precision=HIGH).reshape(rows_x, 3, cols_y)
    bottom_force = jnp.einsum("kr,kf->rf", meet, -force, precision=HIGH).reshape(rows_x, 3, cols_y)
    forcing = source.at[:, 0:3].add(jnp.transpose(bottom_force, (1, 0, 2))[None])
    forcing = forcing.at[:, depth - 1].add(top_force[:, 0][None])
    forcing = forcing.at[:, depth - 2].add(top_force[:, 1][None])
    forcing = forcing.at[:, depth - 3].add(top_force[:, 2][None])
    spectrum = to_modes(forcing, table_z, table_x, table_y)
    modes_new = (scale_now * modes_now[0] - modes_old[0] + scale_spec * spectrum[0])[None]
    pressure_next = to_cells(modes_new, table_z, table_x, table_y)
    return (modes_new, pressure_next)


def solution(mesh):
    placed = (
        P("grp", ("gx", "gy"), None, None),
        P("grp", ("gx", "gy"), None, None),
        P("grp", None, "gx", "gy"),
        P("grp", None, "gx", "gy"),
        P("grp", "gx", "gy"),
        P("grp", "gx", "gy"),
    )
    return jax.shard_map(
        shards,
        mesh=mesh,
        in_specs=placed,
        out_specs=(P("grp", ("gx", "gy"), None, None), P("grp", None, "gx", "gy")),
        check_vma=False,
    )
```

```python
import jax
import jax.numpy as jnp
from jax import lax
from jax.sharding import PartitionSpec as P

COURANT = 0.5
WEIGHTS = (1.5, -0.15, 2.0 / 180.0)
HIGH = lax.Precision.HIGHEST
FAST = lax.Precision.HIGH


def cosine_table(count):
    rows = jnp.arange(count, dtype=jnp.int32).astype(jnp.float32)[:, None]
    cols = jnp.arange(count, dtype=jnp.int32).astype(jnp.float32)[None, :]
    scale = jnp.where(rows == 0, jnp.sqrt(1.0 / count), jnp.sqrt(2.0 / count))
    return scale * jnp.cos(jnp.pi * rows * (cols + 0.5) / count)


def face_stencil(diff):
    first = diff[..., 0, :]
    second = diff[..., 1, :]
    third = diff[..., 2, :]
    return jnp.stack(
        [
            WEIGHTS[0] * first + WEIGHTS[1] * second + WEIGHTS[2] * third,
            WEIGHTS[1] * first + WEIGHTS[2] * second,
            WEIGHTS[2] * first,
        ],
        axis=-2,
    )


def to_modes(field, table_z, table_x, table_y):
    width_x = lax.axis_size("gx")
    width_y = lax.axis_size("gy")
    rows_x = field.shape[2]
    cols_y = field.shape[3]
    part = jnp.einsum("kz,zxy->kxy", table_z, field[0], precision=HIGH)
    part = lax.all_to_all(part, ("gx", "gy"), split_axis=0, concat_axis=0, tiled=True)
    part = part.reshape(width_x, width_y, rows_x, cols_y)
    split_x = table_x.reshape(table_x.shape[0], width_x, rows_x)
    split_y = table_y.reshape(table_y.shape[0], width_y, cols_y)
    part = jnp.einsum("bix,ijxy->bjy", split_x, part, precision=FAST)
    return jnp.einsum("cjy,bjy->bc", split_y, part, precision=FAST)[None, None]


def to_cells(modes, table_z, table_x, table_y):
    width_x = lax.axis_size("gx")
    width_y = lax.axis_size("gy")
    rows_x = modes.shape[2] // width_x
    cols_y = modes.shape[3] // width_y
    split_x = table_x.reshape(table_x.shape[0], width_x, rows_x)
    split_y = table_y.reshape(table_y.shape[0], width_y, cols_y)
    part = jnp.einsum("cjy,bc->bjy", split_y, modes[0, 0], precision=FAST)
    part = jnp.einsum("bix,bjy->ijxy", split_x, part, precision=FAST)
    part = part.reshape(width_x * width_y, rows_x, cols_y)
    cells = lax.all_to_all(part, ("gx", "gy"), split_axis=0, concat_axis=0, tiled=True)
    return jnp.einsum("kz,kxy->zxy", table_z, cells, precision=HIGH)[None]


def advance_terms(depth_index, depth, long_x, long_y):
    index_x = jnp.arange(long_x, dtype=jnp.int32).astype(jnp.float32)
    index_y = jnp.arange(long_y, dtype=jnp.int32).astype(jnp.float32)
    part_z = depth_index / depth * (depth_index / depth)
    part_x = index_x / long_x * (index_x / long_x)
    part_y = index_y / long_y * (index_y / long_y)
    theta = (
        COURANT
        * jnp.pi
        * jnp.sqrt(part_z[:, None, None] + part_x[None, :, None] + part_y[None, None, :])
    )
    shape = jnp.sinc(theta / (2.0 * jnp.pi))
    return 2.0 * jnp.cos(theta), COURANT * COURANT * shape * shape


def lane_stencil(diff, cols):
    first = diff[:, :cols]
    second = diff[:, cols : 2 * cols]
    third = diff[:, 2 * cols :]
    return jnp.concatenate(
        [
            WEIGHTS[0] * first + WEIGHTS[1] * second + WEIGHTS[2] * third,
            WEIGHTS[1] * first + WEIGHTS[2] * second,
            WEIGHTS[2] * first,
        ],
        axis=1,
    )


def one_hot(index, count):
    return (index[:, None] == jnp.arange(count, dtype=jnp.int32)[None, :]).astype(jnp.float32)


def shards(modes_now, modes_old, pressure_now, source, strip_slot, strip_row):
    depth = source.shape[1]
    rows_x = source.shape[2]
    cols_y = source.shape[3]
    planes = modes_now.shape[1]
    long_x = modes_now.shape[2]
    long_y = modes_now.shape[3]
    block = lax.axis_index(("gx", "gy"))
    depth_index = (block * planes + jnp.arange(planes, dtype=jnp.int32)).astype(jnp.float32)
    table_z = lax.optimization_barrier(cosine_table(depth))
    table_x = lax.optimization_barrier(cosine_table(long_x))
    table_y = lax.optimization_barrier(cosine_table(long_y))
    scale_now, scale_spec = advance_terms(depth_index, depth, long_x, long_y)
    scale_now = lax.optimization_barrier(scale_now)
    scale_spec = lax.optimization_barrier(scale_spec)
    top = jnp.stack(
        [pressure_now[0, depth - 1], pressure_now[0, depth - 2], pressure_now[0, depth - 3]], axis=1
    ).reshape(rows_x, 3 * cols_y)
    bottom = jnp.transpose(pressure_now[0, 0:3], (1, 0, 2)).reshape(rows_x, 3 * cols_y)
    every = ("grp", "gx", "gy")
    devices = lax.axis_size(every)
    slots_per = max(2, rows_x // devices)
    total = devices * slots_per
    slots = strip_slot.reshape(-1)
    codes = lax.all_gather(slots * rows_x + strip_row.reshape(-1), every, tiled=True)
    codes = codes.reshape(devices, rows_x)
    want = lax.axis_index(every) * slots_per + jnp.arange(slots_per, dtype=jnp.int32)
    hit = (codes // rows_x)[:, :, None] == want[None, None, :]
    found = jnp.any(hit, axis=1).reshape(total)
    marks = jnp.sum(jnp.where(hit, (codes % rows_x)[:, :, None], 0), axis=1).reshape(total)
    marks = jnp.where(found, marks, -1)
    send = one_hot(slots, total)
    meet = one_hot(marks, rows_x)
    rims_out = jnp.einsum("sk,sf->kf", send, top, precision=HIGH)
    met = jnp.einsum("kr,rf->kf", meet, bottom, precision=HIGH)
    got = lax.all_to_all(
        jnp.concatenate([rims_out, met], axis=1), every, split_axis=0, concat_axis=0, tiled=True
    )
    rims = got[:, : 3 * cols_y]
    far = got[:, 3 * cols_y :]
    live = found.astype(jnp.float32)[:, None]
    force = lane_stencil(met - rims, cols_y) * live
    bottom_force = jnp.einsum("kr,kf->rf", meet, -force, precision=HIGH).reshape(rows_x, 3, cols_y)
    partner = jnp.einsum("sk,kf->sf", send, far, precision=HIGH)
    top_force = lane_stencil(partner - top, cols_y).reshape(rows_x, 3, cols_y)
    forcing = source.at[:, 0:3].add(jnp.transpose(bottom_force, (1, 0, 2))[None])
    forcing = forcing.at[:, depth - 1].add(top_force[:, 0][None])
    forcing = forcing.at[:, depth - 2].add(top_force[:, 1][None])
    forcing = forcing.at[:, depth - 3].add(top_force[:, 2][None])
    spectrum = to_modes(forcing, table_z, table_x, table_y)
    modes_new = (scale_now * modes_now[0] - modes_old[0] + scale_spec * spectrum[0])[None]
    pressure_next = to_cells(modes_new, table_z, table_x, table_y)
    return (modes_new, pressure_next)


def solution(mesh):
    placed = (
        P("grp", ("gx", "gy"), None, None),
        P("grp", ("gx", "gy"), None, None),
        P("grp", None, "gx", "gy"),
        P("grp", None, "gx", "gy"),
        P("grp", "gx", "gy"),
        P("grp", "gx", "gy"),
    )
    return jax.shard_map(
        shards,
        mesh=mesh,
        in_specs=placed,
        out_specs=(P("grp", ("gx", "gy"), None, None), P("grp", None, "gx", "gy")),
        check_vma=False,
    )
```

```python
import jax
import jax.numpy as jnp
from jax import lax
from jax.sharding import PartitionSpec as P

COURANT = 0.5
WEIGHTS = (1.5, -0.15, 2.0 / 180.0)
HIGH = lax.Precision.HIGHEST
FAST = lax.Precision.HIGH


def cosine_table(count):
    rows = jnp.arange(count, dtype=jnp.int32).astype(jnp.float32)[:, None]
    cols = jnp.arange(count, dtype=jnp.int32).astype(jnp.float32)[None, :]
    scale = jnp.where(rows == 0, jnp.sqrt(1.0 / count), jnp.sqrt(2.0 / count))
    return scale * jnp.cos(jnp.pi * rows * (cols + 0.5) / count)


def face_stencil(diff):
    first = diff[..., 0, :]
    second = diff[..., 1, :]
    third = diff[..., 2, :]
    return jnp.stack(
        [
            WEIGHTS[0] * first + WEIGHTS[1] * second + WEIGHTS[2] * third,
            WEIGHTS[1] * first + WEIGHTS[2] * second,
            WEIGHTS[2] * first,
        ],
        axis=-2,
    )


def to_modes(field, table_z, table_x, table_y):
    width_x = lax.axis_size("gx")
    width_y = lax.axis_size("gy")
    rows_x = field.shape[2]
    cols_y = field.shape[3]
    part = jnp.einsum("kz,zxy->kxy", table_z, field[0], precision=HIGH)
    part = lax.all_to_all(part, ("gx", "gy"), split_axis=0, concat_axis=0, tiled=True)
    part = part.reshape(width_x, width_y, rows_x, cols_y)
    split_x = table_x.reshape(table_x.shape[0], width_x, rows_x)
    split_y = table_y.reshape(table_y.shape[0], width_y, cols_y)
    part = jnp.einsum("bix,ijxy->bjy", split_x, part, precision=FAST)
    return jnp.einsum("cjy,bjy->bc", split_y, part, precision=FAST)[None, None]


def to_cells(modes, table_z, table_x, table_y):
    width_x = lax.axis_size("gx")
    width_y = lax.axis_size("gy")
    rows_x = modes.shape[2] // width_x
    cols_y = modes.shape[3] // width_y
    split_x = table_x.reshape(table_x.shape[0], width_x, rows_x)
    split_y = table_y.reshape(table_y.shape[0], width_y, cols_y)
    part = jnp.einsum("cjy,bc->bjy", split_y, modes[0, 0], precision=FAST)
    part = jnp.einsum("bix,bjy->ijxy", split_x, part, precision=FAST)
    part = part.reshape(width_x * width_y, rows_x, cols_y)
    cells = lax.all_to_all(part, ("gx", "gy"), split_axis=0, concat_axis=0, tiled=True)
    return jnp.einsum("kz,kxy->zxy", table_z, cells, precision=HIGH)[None]


def advance_terms(depth_index, depth, long_x, long_y):
    index_x = jnp.arange(long_x, dtype=jnp.int32).astype(jnp.float32)
    index_y = jnp.arange(long_y, dtype=jnp.int32).astype(jnp.float32)
    part_z = depth_index / depth * (depth_index / depth)
    part_x = index_x / long_x * (index_x / long_x)
    part_y = index_y / long_y * (index_y / long_y)
    theta = (
        COURANT
        * jnp.pi
        * jnp.sqrt(part_z[:, None, None] + part_x[None, :, None] + part_y[None, None, :])
    )
    shape = jnp.sinc(theta / (2.0 * jnp.pi))
    return 2.0 * jnp.cos(theta), COURANT * COURANT * shape * shape


def lane_stencil(diff, cols):
    first = diff[:, :cols]
    second = diff[:, cols : 2 * cols]
    third = diff[:, 2 * cols :]
    return jnp.concatenate(
        [
            WEIGHTS[0] * first + WEIGHTS[1] * second + WEIGHTS[2] * third,
            WEIGHTS[1] * first + WEIGHTS[2] * second,
            WEIGHTS[2] * first,
        ],
        axis=1,
    )


def one_hot(index, count):
    return (index[:, None] == jnp.arange(count, dtype=jnp.int32)[None, :]).astype(jnp.float32)


def shards(modes_now, modes_old, pressure_now, source, strip_slot, strip_row):
    depth = source.shape[1]
    rows_x = source.shape[2]
    cols_y = source.shape[3]
    planes = modes_now.shape[1]
    long_x = modes_now.shape[2]
    long_y = modes_now.shape[3]
    block = lax.axis_index(("gx", "gy"))
    depth_index = (block * planes + jnp.arange(planes, dtype=jnp.int32)).astype(jnp.float32)
    table_z = lax.optimization_barrier(cosine_table(depth))
    table_x = lax.optimization_barrier(cosine_table(long_x))
    table_y = lax.optimization_barrier(cosine_table(long_y))
    scale_now, scale_spec = advance_terms(depth_index, depth, long_x, long_y)
    scale_now = lax.optimization_barrier(scale_now)
    scale_spec = lax.optimization_barrier(scale_spec)
    top = jnp.stack(
        [pressure_now[0, depth - 1], pressure_now[0, depth - 2], pressure_now[0, depth - 3]], axis=1
    ).reshape(rows_x, 3 * cols_y)
    bottom = jnp.transpose(pressure_now[0, 0:3], (1, 0, 2)).reshape(rows_x, 3 * cols_y)
    every = ("grp", "gx", "gy")
    devices = lax.axis_size(every)
    slots_per = max(2, rows_x // devices)
    total = devices * slots_per
    slots = strip_slot.reshape(-1)
    mine = (slots * rows_x + strip_row.reshape(-1)).astype(jnp.float32)
    owner = jnp.arange(devices, dtype=jnp.int32)[:, None] == lax.axis_index(every)
    codes = lax.psum(jnp.where(owner, mine[None, :], 0.0), every)
    codes = jnp.round(codes).astype(jnp.int32)
    want = lax.axis_index(every) * slots_per + jnp.arange(slots_per, dtype=jnp.int32)
    hit = (codes // rows_x)[:, :, None] == want[None, None, :]
    found = jnp.any(hit, axis=1).reshape(total)
    marks = jnp.sum(jnp.where(hit, (codes % rows_x)[:, :, None], 0), axis=1).reshape(total)
    marks = jnp.where(found, marks, -1)
    send = one_hot(slots, total)
    meet = one_hot(marks, rows_x)
    rims_out = jnp.einsum("sk,sf->kf", send, top, precision=HIGH)
    met = jnp.einsum("kr,rf->kf", meet, bottom, precision=HIGH)
    got = lax.all_to_all(
        jnp.concatenate([rims_out, met], axis=1), every, split_axis=0, concat_axis=0, tiled=True
    )
    rims = got[:, : 3 * cols_y]
    far = got[:, 3 * cols_y :]
    live = found.astype(jnp.float32)[:, None]
    force = lane_stencil(met - rims, cols_y) * live
    bottom_force = jnp.einsum("kr,kf->rf", meet, -force, precision=HIGH).reshape(rows_x, 3, cols_y)
    partner = jnp.einsum("sk,kf->sf", send, far, precision=HIGH)
    top_force = lane_stencil(partner - top, cols_y).reshape(rows_x, 3, cols_y)
    forcing = source.at[:, 0:3].add(jnp.transpose(bottom_force, (1, 0, 2))[None])
    forcing = forcing.at[:, depth - 1].add(top_force[:, 0][None])
    forcing = forcing.at[:, depth - 2].add(top_force[:, 1][None])
    forcing = forcing.at[:, depth - 3].add(top_force[:, 2][None])
    spectrum = to_modes(forcing, table_z, table_x, table_y)
    modes_new = (scale_now * modes_now[0] - modes_old[0] + scale_spec * spectrum[0])[None]
    pressure_next = to_cells(modes_new, table_z, table_x, table_y)
    return (modes_new, pressure_next)


def solution(mesh):
    placed = (
        P("grp", ("gx", "gy"), None, None),
        P("grp", ("gx", "gy"), None, None),
        P("grp", None, "gx", "gy"),
        P("grp", None, "gx", "gy"),
        P("grp", "gx", "gy"),
        P("grp", "gx", "gy"),
    )
    return jax.shard_map(
        shards,
        mesh=mesh,
        in_specs=placed,
        out_specs=(P("grp", ("gx", "gy"), None, None), P("grp", None, "gx", "gy")),
        check_vma=False,
    )
```

```python
import jax
import jax.numpy as jnp
from jax import lax
from jax.sharding import PartitionSpec as P

COURANT = 0.5
WEIGHTS = (1.5, -0.15, 2.0 / 180.0)
HIGH = lax.Precision.HIGHEST
FAST = lax.Precision.HIGH


def cosine_table(count):
    rows = jnp.arange(count, dtype=jnp.int32).astype(jnp.float32)[:, None]
    cols = jnp.arange(count, dtype=jnp.int32).astype(jnp.float32)[None, :]
    scale = jnp.where(rows == 0, jnp.sqrt(1.0 / count), jnp.sqrt(2.0 / count))
    return scale * jnp.cos(jnp.pi * rows * (cols + 0.5) / count)


def face_stencil(diff):
    first = diff[..., 0, :]
    second = diff[..., 1, :]
    third = diff[..., 2, :]
    return jnp.stack(
        [
            WEIGHTS[0] * first + WEIGHTS[1] * second + WEIGHTS[2] * third,
            WEIGHTS[1] * first + WEIGHTS[2] * second,
            WEIGHTS[2] * first,
        ],
        axis=-2,
    )


def to_modes(zsource, layers, table_edge, table_x, table_y):
    width_x = lax.axis_size("gx")
    width_y = lax.axis_size("gy")
    rows_x = zsource.shape[1]
    cols_y = zsource.shape[2]
    part = zsource + jnp.einsum("kz,zxy->kxy", table_edge, layers, precision=HIGH)
    part = lax.all_to_all(part, ("gx", "gy"), split_axis=0, concat_axis=0, tiled=True)
    part = part.reshape(width_x, width_y, rows_x, cols_y)
    split_x = table_x.reshape(table_x.shape[0], width_x, rows_x)
    split_y = table_y.reshape(table_y.shape[0], width_y, cols_y)
    part = jnp.einsum("bix,ijxy->bjy", split_x, part, precision=FAST)
    return jnp.einsum("cjy,bjy->bc", split_y, part, precision=FAST)[None, None]


def to_cells(modes, table_z, table_x, table_y):
    width_x = lax.axis_size("gx")
    width_y = lax.axis_size("gy")
    rows_x = modes.shape[2] // width_x
    cols_y = modes.shape[3] // width_y
    split_y = table_y.reshape(table_y.shape[0], width_y, cols_y)
    part = jnp.einsum("cjy,bc->jby", split_y, modes[0, 0], precision=FAST)
    part = jnp.einsum("bn,jby->jny", table_x, part, precision=FAST)
    part = part.reshape(width_x * width_y, rows_x, cols_y)
    cells = lax.all_to_all(part, ("gy", "gx"), split_axis=0, concat_axis=0, tiled=True)
    depth = table_z.shape[1]
    table_p = table_z.reshape(width_x, width_y, depth).transpose(1, 0, 2).reshape(-1, depth)
    return jnp.einsum("kz,kxy->zxy", table_p, cells, precision=HIGH)[None]


def advance_terms(depth_index, depth, long_x, long_y):
    index_x = jnp.arange(long_x, dtype=jnp.int32).astype(jnp.float32)
    index_y = jnp.arange(long_y, dtype=jnp.int32).astype(jnp.float32)
    part_z = depth_index / depth * (depth_index / depth)
    part_x = index_x / long_x * (index_x / long_x)
    part_y = index_y / long_y * (index_y / long_y)
    theta = (
        COURANT
        * jnp.pi
        * jnp.sqrt(part_z[:, None, None] + part_x[None, :, None] + part_y[None, None, :])
    )
    shape = jnp.sinc(theta / (2.0 * jnp.pi))
    return 2.0 * jnp.cos(theta), COURANT * COURANT * shape * shape


def one_hot(index, count):
    return (index[:, None] == jnp.arange(count, dtype=jnp.int32)[None, :]).astype(jnp.float32)


def shards(modes_now, modes_old, pressure_now, source, strip_slot, strip_row):
    depth = source.shape[1]
    rows_x = source.shape[2]
    cols_y = source.shape[3]
    planes = modes_now.shape[1]
    long_x = modes_now.shape[2]
    long_y = modes_now.shape[3]
    block = lax.axis_index(("gx", "gy"))
    depth_index = (block * planes + jnp.arange(planes, dtype=jnp.int32)).astype(jnp.float32)
    table_z = lax.optimization_barrier(cosine_table(depth))
    table_x = lax.optimization_barrier(cosine_table(long_x))
    table_y = lax.optimization_barrier(cosine_table(long_y))
    scale_now, scale_spec = advance_terms(depth_index, depth, long_x, long_y)
    base = lax.optimization_barrier(scale_now * modes_now[0] - modes_old[0])
    scale_spec = lax.optimization_barrier(scale_spec)
    zsource = lax.optimization_barrier(
        jnp.einsum("kz,zxy->kxy", table_z, source[0], precision=HIGH)
    )
    top = jnp.stack(
        [pressure_now[0, depth - 1], pressure_now[0, depth - 2], pressure_now[0, depth - 3]], axis=1
    ).reshape(rows_x, 3 * cols_y)
    bottom = jnp.transpose(pressure_now[0, 0:3], (1, 0, 2)).reshape(rows_x, 3 * cols_y)
    devices = lax.axis_size(("grp", "gx", "gy"))
    slots_per = max(2, rows_x // devices)
    total = devices * slots_per
    slots = strip_slot.reshape(-1)
    rows = strip_row.reshape(-1)
    label = jnp.broadcast_to((rows + 1).astype(jnp.float32)[:, None], (rows_x, cols_y))
    send = one_hot(slots, total)
    payload = jnp.concatenate([top, label], axis=1)
    buffer = jnp.einsum("sk,sf->kf", send, payload, precision=HIGH)
    got = lax.all_to_all(buffer, ("grp", "gx", "gy"), split_axis=0, concat_axis=0, tiled=True)
    rims = got[:, : 3 * cols_y]
    marks = jnp.round(got[:, 3 * cols_y]).astype(jnp.int32) - 1
    live = (marks >= 0).astype(jnp.float32)[:, None]
    meet = one_hot(marks, rows_x)
    met = jnp.einsum("kr,rf->kf", meet, bottom, precision=HIGH)
    diff = met - rims
    first = diff[:, :cols_y]
    second = diff[:, cols_y : 2 * cols_y]
    third = diff[:, 2 * cols_y :]
    force = jnp.concatenate(
        [
            WEIGHTS[0] * first + WEIGHTS[1] * second + WEIGHTS[2] * third,
            WEIGHTS[1] * first + WEIGHTS[2] * second,
            WEIGHTS[2] * first,
        ],
        axis=1,
    ) * live
    back = lax.all_to_all(force, ("grp", "gx", "gy"), split_axis=0, concat_axis=0, tiled=True)
    top_force = jnp.einsum("sk,kf->sf", send, back, precision=HIGH).reshape(rows_x, 3, cols_y)
    bottom_force = jnp.einsum("kr,kf->rf", meet, -force, precision=HIGH).reshape(rows_x, 3, cols_y)
    table_x, top_force = lax.optimization_barrier((table_x, top_force))
    layers = jnp.concatenate(
        [
            jnp.transpose(bottom_force, (1, 0, 2)),
            top_force[:, 2][None],
            top_force[:, 1][None],
            top_force[:, 0][None],
        ],
        axis=0,
    )
    edges = jnp.concatenate([table_z[:, :3], table_z[:, depth - 3 :]], axis=1)
    spectrum = to_modes(zsource, layers, edges, table_x, table_y)
    modes_new = (base + scale_spec * spectrum[0])[None]
    pressure_next = to_cells(modes_new, table_z, table_x, table_y)
    return (modes_new, pressure_next)


def solution(mesh):
    placed = (
        P("grp", ("gx", "gy"), None, None),
        P("grp", ("gx", "gy"), None, None),
        P("grp", None, "gx", "gy"),
        P("grp", None, "gx", "gy"),
        P("grp", "gx", "gy"),
        P("grp", "gx", "gy"),
    )
    return jax.shard_map(
        shards,
        mesh=mesh,
        in_specs=placed,
        out_specs=(P("grp", ("gx", "gy"), None, None), P("grp", None, "gx", "gy")),
        check_vma=False,
    )
```

```python
import jax
import jax.numpy as jnp
from jax import lax
from jax.sharding import PartitionSpec as P

COURANT = 0.5
WEIGHTS = (1.5, -0.15, 2.0 / 180.0)
HIGH = lax.Precision.HIGHEST
FAST = lax.Precision.HIGH


def cosine_table(count):
    rows = jnp.arange(count, dtype=jnp.int32).astype(jnp.float32)[:, None]
    cols = jnp.arange(count, dtype=jnp.int32).astype(jnp.float32)[None, :]
    scale = jnp.where(rows == 0, jnp.sqrt(1.0 / count), jnp.sqrt(2.0 / count))
    return scale * jnp.cos(jnp.pi * rows * (cols + 0.5) / count)


def face_stencil(diff):
    first = diff[..., 0, :]
    second = diff[..., 1, :]
    third = diff[..., 2, :]
    return jnp.stack(
        [
            WEIGHTS[0] * first + WEIGHTS[1] * second + WEIGHTS[2] * third,
            WEIGHTS[1] * first + WEIGHTS[2] * second,
            WEIGHTS[2] * first,
        ],
        axis=-2,
    )


def to_modes(field, table_z, table_x, table_y):
    width_x = lax.axis_size("gx")
    width_y = lax.axis_size("gy")
    rows_x = field.shape[2]
    cols_y = field.shape[3]
    part = jnp.einsum("kz,zxy->kxy", table_z, field[0], precision=HIGH)
    part = lax.all_to_all(part, ("gx", "gy"), split_axis=0, concat_axis=0, tiled=True)
    part = part.reshape(width_x, width_y, rows_x, cols_y)
    split_x = table_x.reshape(table_x.shape[0], width_x, rows_x)
    split_y = table_y.reshape(table_y.shape[0], width_y, cols_y)
    part = jnp.einsum("bix,ijxy->bjy", split_x, part, precision=FAST)
    return jnp.einsum("cjy,bjy->bc", split_y, part, precision=FAST)[None, None]


def to_cells(modes, table_z, table_x, table_y):
    width_x = lax.axis_size("gx")
    width_y = lax.axis_size("gy")
    rows_x = modes.shape[2] // width_x
    cols_y = modes.shape[3] // width_y
    split_x = table_x.reshape(table_x.shape[0], width_x, rows_x)
    split_y = table_y.reshape(table_y.shape[0], width_y, cols_y)
    part = jnp.einsum("cjy,bc->bjy", split_y, modes[0, 0], precision=FAST)
    part = jnp.einsum("bix,bjy->ijxy", split_x, part, precision=FAST)
    part = part.reshape(width_x * width_y, rows_x, cols_y)
    cells = lax.all_to_all(part, ("gx", "gy"), split_axis=0, concat_axis=0, tiled=True)
    return jnp.einsum("kz,kxy->zxy", table_z, cells, precision=HIGH)[None]


def advance_terms(depth_index, depth, long_x, long_y):
    index_x = jnp.arange(long_x, dtype=jnp.int32).astype(jnp.float32)
    index_y = jnp.arange(long_y, dtype=jnp.int32).astype(jnp.float32)
    part_z = depth_index / depth * (depth_index / depth)
    part_x = index_x / long_x * (index_x / long_x)
    part_y = index_y / long_y * (index_y / long_y)
    theta = (
        COURANT
        * jnp.pi
        * jnp.sqrt(part_z[:, None, None] + part_x[None, :, None] + part_y[None, None, :])
    )
    shape = jnp.sinc(theta / (2.0 * jnp.pi))
    return 2.0 * jnp.cos(theta), COURANT * COURANT * shape * shape


def one_hot(index, count):
    return (index[:, None] == jnp.arange(count, dtype=jnp.int32)[None, :]).astype(jnp.float32)


def shards(modes_now, modes_old, pressure_now, source, strip_slot, strip_row):
    depth = source.shape[1]
    rows_x = source.shape[2]
    cols_y = source.shape[3]
    planes = modes_now.shape[1]
    long_x = modes_now.shape[2]
    long_y = modes_now.shape[3]
    block = lax.axis_index(("gx", "gy"))
    depth_index = (block * planes + jnp.arange(planes, dtype=jnp.int32)).astype(jnp.float32)
    table_z = lax.optimization_barrier(cosine_table(depth))
    table_x = lax.optimization_barrier(cosine_table(long_x))
    table_y = lax.optimization_barrier(cosine_table(long_y))
    scale_now, scale_spec = advance_terms(depth_index, depth, long_x, long_y)
    base = lax.optimization_barrier(scale_now * modes_now[0] - modes_old[0])
    scale_spec = lax.optimization_barrier(scale_spec)
    top = jnp.stack(
        [pressure_now[0, depth - 1], pressure_now[0, depth - 2], pressure_now[0, depth - 3]], axis=1
    ).reshape(rows_x, 3 * cols_y)
    bottom = jnp.transpose(pressure_now[0, 0:3], (1, 0, 2)).reshape(rows_x, 3 * cols_y)
    devices = lax.axis_size(("grp", "gx", "gy"))
    slots_per = max(2, rows_x // devices)
    total = devices * slots_per
    slots = strip_slot.reshape(-1)
    rows = strip_row.reshape(-1)
    label = jnp.broadcast_to((rows + 1).astype(jnp.float32)[:, None], (rows_x, cols_y))
    send = one_hot(slots, total)
    payload = jnp.concatenate([top, label], axis=1)
    buffer = jnp.einsum("sk,sf->kf", send, payload, precision=HIGH)
    got = lax.all_to_all(buffer, ("grp", "gx", "gy"), split_axis=0, concat_axis=0, tiled=True)
    rims = got[:, : 3 * cols_y]
    marks = jnp.round(got[:, 3 * cols_y]).astype(jnp.int32) - 1
    live = (marks >= 0).astype(jnp.float32)[:, None]
    meet = one_hot(marks, rows_x)
    met = jnp.einsum("kr,rf->kf", meet, bottom, precision=HIGH)
    diff = met - rims
    first = diff[:, :cols_y]
    second = diff[:, cols_y : 2 * cols_y]
    third = diff[:, 2 * cols_y :]
    force = jnp.concatenate(
        [
            WEIGHTS[0] * first + WEIGHTS[1] * second + WEIGHTS[2] * third,
            WEIGHTS[1] * first + WEIGHTS[2] * second,
            WEIGHTS[2] * first,
        ],
        axis=1,
    ) * live
    back = lax.all_to_all(force, ("grp", "gx", "gy"), split_axis=0, concat_axis=0, tiled=True)
    top_force = jnp.einsum("sk,kf->sf", send, back, precision=HIGH).reshape(rows_x, 3, cols_y)
    bottom_force = jnp.einsum("kr,kf->rf", meet, -force, precision=HIGH).reshape(rows_x, 3, cols_y)
    forcing = source.at[:, 0:3].add(jnp.transpose(bottom_force, (1, 0, 2))[None])
    forcing = forcing.at[:, depth - 1].add(top_force[:, 0][None])
    forcing = forcing.at[:, depth - 2].add(top_force[:, 1][None])
    forcing = forcing.at[:, depth - 3].add(top_force[:, 2][None])
    spectrum = to_modes(forcing, table_z, table_x, table_y)
    modes_new = (base + scale_spec * spectrum[0])[None]
    pressure_next = to_cells(modes_new, table_z, table_x, table_y)
    return (modes_new, pressure_next)


def solution(mesh):
    placed = (
        P("grp", ("gx", "gy"), None, None),
        P("grp", ("gx", "gy"), None, None),
        P("grp", None, "gx", "gy"),
        P("grp", None, "gx", "gy"),
        P("grp", "gx", "gy"),
        P("grp", "gx", "gy"),
    )
    return jax.shard_map(
        shards,
        mesh=mesh,
        in_specs=placed,
        out_specs=(P("grp", ("gx", "gy"), None, None), P("grp", None, "gx", "gy")),
        check_vma=False,
    )
```

```python
import jax
import jax.numpy as jnp
from jax import lax
from jax.sharding import PartitionSpec as P

COURANT = 0.5
WEIGHTS = (1.5, -0.15, 2.0 / 180.0)
HIGH = lax.Precision.HIGHEST
FAST = lax.Precision.HIGH


def cosine_table(count):
    rows = jnp.arange(count, dtype=jnp.int32).astype(jnp.float32)[:, None]
    cols = jnp.arange(count, dtype=jnp.int32).astype(jnp.float32)[None, :]
    scale = jnp.where(rows == 0, jnp.sqrt(1.0 / count), jnp.sqrt(2.0 / count))
    return scale * jnp.cos(jnp.pi * rows * (cols + 0.5) / count)


def face_stencil(diff):
    first = diff[..., 0, :]
    second = diff[..., 1, :]
    third = diff[..., 2, :]
    return jnp.stack(
        [
            WEIGHTS[0] * first + WEIGHTS[1] * second + WEIGHTS[2] * third,
            WEIGHTS[1] * first + WEIGHTS[2] * second,
            WEIGHTS[2] * first,
        ],
        axis=-2,
    )


def to_modes(field, table_z, table_x, table_y):
    width_x = lax.axis_size("gx")
    width_y = lax.axis_size("gy")
    rows_x = field.shape[2]
    cols_y = field.shape[3]
    part = jnp.einsum("kz,zxy->kxy", table_z, field[0], precision=FAST)
    part = lax.all_to_all(part, ("gx", "gy"), split_axis=0, concat_axis=0, tiled=True)
    part = part.reshape(width_x, width_y, rows_x, cols_y)
    split_x = table_x.reshape(table_x.shape[0], width_x, rows_x)
    split_y = table_y.reshape(table_y.shape[0], width_y, cols_y)
    part = jnp.einsum("bix,ijxy->bjy", split_x, part, precision=FAST)
    return jnp.einsum("cjy,bjy->bc", split_y, part, precision=FAST)[None, None]


def to_cells(modes, table_z, table_x, table_y):
    width_x = lax.axis_size("gx")
    width_y = lax.axis_size("gy")
    rows_x = modes.shape[2] // width_x
    cols_y = modes.shape[3] // width_y
    split_x = table_x.reshape(table_x.shape[0], width_x, rows_x)
    split_y = table_y.reshape(table_y.shape[0], width_y, cols_y)
    part = jnp.einsum("cjy,bc->bjy", split_y, modes[0, 0], precision=FAST)
    part = jnp.einsum("bix,bjy->ijxy", split_x, part, precision=FAST)
    part = part.reshape(width_x * width_y, rows_x, cols_y)
    cells = lax.all_to_all(part, ("gx", "gy"), split_axis=0, concat_axis=0, tiled=True)
    return jnp.einsum("kz,kxy->zxy", table_z, cells, precision=FAST)[None]


def advance_terms(depth_index, depth, long_x, long_y):
    index_x = jnp.arange(long_x, dtype=jnp.int32).astype(jnp.float32)
    index_y = jnp.arange(long_y, dtype=jnp.int32).astype(jnp.float32)
    part_z = depth_index / depth * (depth_index / depth)
    part_x = index_x / long_x * (index_x / long_x)
    part_y = index_y / long_y * (index_y / long_y)
    theta = (
        COURANT
        * jnp.pi
        * jnp.sqrt(part_z[:, None, None] + part_x[None, :, None] + part_y[None, None, :])
    )
    shape = jnp.sinc(theta / (2.0 * jnp.pi))
    return 2.0 * jnp.cos(theta), COURANT * COURANT * shape * shape


def one_hot(index, count):
    return (index[:, None] == jnp.arange(count, dtype=jnp.int32)[None, :]).astype(jnp.float32)


def shards(modes_now, modes_old, pressure_now, source, strip_slot, strip_row):
    depth = source.shape[1]
    rows_x = source.shape[2]
    cols_y = source.shape[3]
    planes = modes_now.shape[1]
    long_x = modes_now.shape[2]
    long_y = modes_now.shape[3]
    block = lax.axis_index(("gx", "gy"))
    depth_index = (block * planes + jnp.arange(planes, dtype=jnp.int32)).astype(jnp.float32)
    table_z = lax.optimization_barrier(cosine_table(depth))
    table_x = lax.optimization_barrier(cosine_table(long_x))
    table_y = lax.optimization_barrier(cosine_table(long_y))
    scale_now, scale_spec = advance_terms(depth_index, depth, long_x, long_y)
    scale_now = lax.optimization_barrier(scale_now)
    scale_spec = lax.optimization_barrier(scale_spec)
    top = jnp.stack(
        [pressure_now[0, depth - 1], pressure_now[0, depth - 2], pressure_now[0, depth - 3]], axis=1
    ).reshape(rows_x, 3 * cols_y)
    bottom = jnp.transpose(pressure_now[0, 0:3], (1, 0, 2)).reshape(rows_x, 3 * cols_y)
    devices = lax.axis_size(("grp", "gx", "gy"))
    slots_per = max(2, rows_x // devices)
    total = devices * slots_per
    slots = strip_slot.reshape(-1)
    rows = strip_row.reshape(-1)
    label = jnp.broadcast_to((rows + 1).astype(jnp.float32)[:, None], (rows_x, cols_y))
    send = one_hot(slots, total)
    payload = jnp.concatenate([top, label], axis=1)
    buffer = jnp.einsum("sk,sf->kf", send, payload, precision=HIGH)
    got = lax.all_to_all(buffer, ("grp", "gx", "gy"), split_axis=0, concat_axis=0, tiled=True)
    rims = got[:, : 3 * cols_y]
    marks = jnp.round(got[:, 3 * cols_y]).astype(jnp.int32) - 1
    live = (marks >= 0).astype(jnp.float32)[:, None]
    meet = one_hot(marks, rows_x)
    met = jnp.einsum("kr,rf->kf", meet, bottom, precision=HIGH)
    diff = met - rims
    first = diff[:, :cols_y]
    second = diff[:, cols_y : 2 * cols_y]
    third = diff[:, 2 * cols_y :]
    force = jnp.concatenate(
        [
            WEIGHTS[0] * first + WEIGHTS[1] * second + WEIGHTS[2] * third,
            WEIGHTS[1] * first + WEIGHTS[2] * second,
            WEIGHTS[2] * first,
        ],
        axis=1,
    ) * live
    back = lax.all_to_all(force, ("grp", "gx", "gy"), split_axis=0, concat_axis=0, tiled=True)
    top_force = jnp.einsum("sk,kf->sf", send, back, precision=HIGH).reshape(rows_x, 3, cols_y)
    bottom_force = jnp.einsum("kr,kf->rf", meet, -force, precision=HIGH).reshape(rows_x, 3, cols_y)
    forcing = source.at[:, 0:3].add(jnp.transpose(bottom_force, (1, 0, 2))[None])
    forcing = forcing.at[:, depth - 1].add(top_force[:, 0][None])
    forcing = forcing.at[:, depth - 2].add(top_force[:, 1][None])
    forcing = forcing.at[:, depth - 3].add(top_force[:, 2][None])
    spectrum = to_modes(forcing, table_z, table_x, table_y)
    modes_new = (scale_now * modes_now[0] - modes_old[0] + scale_spec * spectrum[0])[None]
    pressure_next = to_cells(modes_new, table_z, table_x, table_y)
    return (modes_new, pressure_next)


def solution(mesh):
    placed = (
        P("grp", ("gx", "gy"), None, None),
        P("grp", ("gx", "gy"), None, None),
        P("grp", None, "gx", "gy"),
        P("grp", None, "gx", "gy"),
        P("grp", "gx", "gy"),
        P("grp", "gx", "gy"),
    )
    return jax.shard_map(
        shards,
        mesh=mesh,
        in_specs=placed,
        out_specs=(P("grp", ("gx", "gy"), None, None), P("grp", None, "gx", "gy")),
        check_vma=False,
    )
```

```python
import jax
import jax.numpy as jnp
from jax import lax
from jax.sharding import PartitionSpec as P

COURANT = 0.5
WEIGHTS = (1.5, -0.15, 2.0 / 180.0)
HIGH = lax.Precision.HIGHEST
FAST = lax.Precision.HIGH


def cosine_table(count):
    rows = jnp.arange(count, dtype=jnp.int32).astype(jnp.float32)[:, None]
    cols = jnp.arange(count, dtype=jnp.int32).astype(jnp.float32)[None, :]
    scale = jnp.where(rows == 0, jnp.sqrt(1.0 / count), jnp.sqrt(2.0 / count))
    return scale * jnp.cos(jnp.pi * rows * (cols + 0.5) / count)


def face_stencil(diff):
    first = diff[..., 0, :]
    second = diff[..., 1, :]
    third = diff[..., 2, :]
    return jnp.stack(
        [
            WEIGHTS[0] * first + WEIGHTS[1] * second + WEIGHTS[2] * third,
            WEIGHTS[1] * first + WEIGHTS[2] * second,
            WEIGHTS[2] * first,
        ],
        axis=-2,
    )


def to_modes(field, table_z, table_x, table_y):
    width_x = lax.axis_size("gx")
    width_y = lax.axis_size("gy")
    rows_x = field.shape[2]
    cols_y = field.shape[3]
    part = jnp.einsum("kz,zxy->kxy", table_z, field[0], precision=FAST)
    part = lax.all_to_all(part, ("gx", "gy"), split_axis=0, concat_axis=0, tiled=True)
    part = part.reshape(width_x, width_y, rows_x, cols_y)
    split_x = table_x.reshape(table_x.shape[0], width_x, rows_x)
    split_y = table_y.reshape(table_y.shape[0], width_y, cols_y)
    part = jnp.einsum("bix,ijxy->bjy", split_x, part, precision=FAST)
    return jnp.einsum("cjy,bjy->bc", split_y, part, precision=FAST)[None, None]


def to_cells(modes, table_z, table_x, table_y):
    width_x = lax.axis_size("gx")
    width_y = lax.axis_size("gy")
    rows_x = modes.shape[2] // width_x
    cols_y = modes.shape[3] // width_y
    split_x = table_x.reshape(table_x.shape[0], width_x, rows_x)
    split_y = table_y.reshape(table_y.shape[0], width_y, cols_y)
    part = jnp.einsum("cjy,bc->bjy", split_y, modes[0, 0], precision=FAST)
    part = jnp.einsum("bix,bjy->ijxy", split_x, part, precision=FAST)
    part = part.reshape(width_x * width_y, rows_x, cols_y)
    cells = lax.all_to_all(part, ("gx", "gy"), split_axis=0, concat_axis=0, tiled=True)
    return jnp.einsum("kz,kxy->zxy", table_z, cells, precision=FAST)[None]


def advance_terms(depth_index, depth, long_x, long_y):
    index_x = jnp.arange(long_x, dtype=jnp.int32).astype(jnp.float32)
    index_y = jnp.arange(long_y, dtype=jnp.int32).astype(jnp.float32)
    part_z = depth_index / depth * (depth_index / depth)
    part_x = index_x / long_x * (index_x / long_x)
    part_y = index_y / long_y * (index_y / long_y)
    theta = (
        COURANT
        * jnp.pi
        * jnp.sqrt(part_z[:, None, None] + part_x[None, :, None] + part_y[None, None, :])
    )
    shape = jnp.sinc(theta / (2.0 * jnp.pi))
    return 2.0 * jnp.cos(theta), COURANT * COURANT * shape * shape


def one_hot(index, count):
    return (index[:, None] == jnp.arange(count, dtype=jnp.int32)[None, :]).astype(jnp.float32)


def shards(modes_now, modes_old, pressure_now, source, strip_slot, strip_row):
    depth = source.shape[1]
    rows_x = source.shape[2]
    cols_y = source.shape[3]
    planes = modes_now.shape[1]
    long_x = modes_now.shape[2]
    long_y = modes_now.shape[3]
    block = lax.axis_index(("gx", "gy"))
    depth_index = (block * planes + jnp.arange(planes, dtype=jnp.int32)).astype(jnp.float32)
    table_z = lax.optimization_barrier(cosine_table(depth))
    table_x = lax.optimization_barrier(cosine_table(long_x))
    table_y = lax.optimization_barrier(cosine_table(long_y))
    scale_now, scale_spec = advance_terms(depth_index, depth, long_x, long_y)
    scale_now = lax.optimization_barrier(scale_now)
    scale_spec = lax.optimization_barrier(scale_spec)
    top = jnp.stack(
        [pressure_now[0, depth - 1], pressure_now[0, depth - 2], pressure_now[0, depth - 3]], axis=1
    ).reshape(rows_x, 3 * cols_y)
    bottom = jnp.transpose(pressure_now[0, 0:3], (1, 0, 2)).reshape(rows_x, 3 * cols_y)
    devices = lax.axis_size(("grp", "gx", "gy"))
    slots_per = max(2, rows_x // devices)
    total = devices * slots_per
    slots = strip_slot.reshape(-1)
    rows = strip_row.reshape(-1)
    label = jnp.broadcast_to((rows + 1).astype(jnp.float32)[:, None], (rows_x, cols_y))
    send = one_hot(slots, total)
    payload = jnp.concatenate([top, label], axis=1)
    buffer = jnp.einsum("sk,sf->kf", send, payload, precision=HIGH)
    got = lax.all_to_all(buffer, ("grp", "gx", "gy"), split_axis=0, concat_axis=0, tiled=True)
    rims = got[:, : 3 * cols_y]
    marks = jnp.round(got[:, 3 * cols_y]).astype(jnp.int32) - 1
    marks, scale_now, scale_spec = lax.optimization_barrier((marks, scale_now, scale_spec))
    live = (marks >= 0).astype(jnp.float32)[:, None]
    meet = one_hot(marks, rows_x)
    met = jnp.einsum("kr,rf->kf", meet, bottom, precision=HIGH)
    diff = met - rims
    first = diff[:, :cols_y]
    second = diff[:, cols_y : 2 * cols_y]
    third = diff[:, 2 * cols_y :]
    force = jnp.concatenate(
        [
            WEIGHTS[0] * first + WEIGHTS[1] * second + WEIGHTS[2] * third,
            WEIGHTS[1] * first + WEIGHTS[2] * second,
            WEIGHTS[2] * first,
        ],
        axis=1,
    ) * live
    back = lax.all_to_all(force, ("grp", "gx", "gy"), split_axis=0, concat_axis=0, tiled=True)
    top_force = jnp.einsum("sk,kf->sf", send, back, precision=HIGH).reshape(rows_x, 3, cols_y)
    bottom_force = jnp.einsum("kr,kf->rf", meet, -force, precision=HIGH).reshape(rows_x, 3, cols_y)
    forcing = source.at[:, 0:3].add(jnp.transpose(bottom_force, (1, 0, 2))[None])
    forcing = forcing.at[:, depth - 1].add(top_force[:, 0][None])
    forcing = forcing.at[:, depth - 2].add(top_force[:, 1][None])
    forcing = forcing.at[:, depth - 3].add(top_force[:, 2][None])
    spectrum = to_modes(forcing, table_z, table_x, table_y)
    modes_new = (scale_now * modes_now[0] - modes_old[0] + scale_spec * spectrum[0])[None]
    pressure_next = to_cells(modes_new, table_z, table_x, table_y)
    return (modes_new, pressure_next)


def solution(mesh):
    placed = (
        P("grp", ("gx", "gy"), None, None),
        P("grp", ("gx", "gy"), None, None),
        P("grp", None, "gx", "gy"),
        P("grp", None, "gx", "gy"),
        P("grp", "gx", "gy"),
        P("grp", "gx", "gy"),
    )
    return jax.shard_map(
        shards,
        mesh=mesh,
        in_specs=placed,
        out_specs=(P("grp", ("gx", "gy"), None, None), P("grp", None, "gx", "gy")),
        check_vma=False,
    )
```

```python
import jax
import jax.numpy as jnp
from jax import lax
from jax.sharding import PartitionSpec as P

COURANT = 0.5
WEIGHTS = (1.5, -0.15, 2.0 / 180.0)
HIGH = lax.Precision.HIGHEST
FAST = lax.Precision.HIGH


def cosine_table(count):
    rows = jnp.arange(count, dtype=jnp.int32).astype(jnp.float32)[:, None]
    cols = jnp.arange(count, dtype=jnp.int32).astype(jnp.float32)[None, :]
    scale = jnp.where(rows == 0, jnp.sqrt(1.0 / count), jnp.sqrt(2.0 / count))
    return scale * jnp.cos(jnp.pi * rows * (cols + 0.5) / count)


def face_stencil(diff):
    first = diff[..., 0, :]
    second = diff[..., 1, :]
    third = diff[..., 2, :]
    return jnp.stack(
        [
            WEIGHTS[0] * first + WEIGHTS[1] * second + WEIGHTS[2] * third,
            WEIGHTS[1] * first + WEIGHTS[2] * second,
            WEIGHTS[2] * first,
        ],
        axis=-2,
    )


def to_modes(field, table_z, table_x, table_y):
    width_x = lax.axis_size("gx")
    width_y = lax.axis_size("gy")
    rows_x = field.shape[2]
    cols_y = field.shape[3]
    part = jnp.einsum("kz,zxy->kxy", table_z, field[0], precision=FAST)
    part = lax.all_to_all(part, ("gx", "gy"), split_axis=0, concat_axis=0, tiled=True)
    part = part.reshape(width_x, width_y, rows_x, cols_y)
    split_x = table_x.reshape(table_x.shape[0], width_x, rows_x)
    split_y = table_y.reshape(table_y.shape[0], width_y, cols_y)
    part = jnp.einsum("bix,ijxy->bjy", split_x, part, precision=FAST)
    return jnp.einsum("cjy,bjy->bc", split_y, part, precision=FAST)[None, None]


def to_cells(modes, table_z, table_x, table_y):
    width_x = lax.axis_size("gx")
    width_y = lax.axis_size("gy")
    rows_x = modes.shape[2] // width_x
    cols_y = modes.shape[3] // width_y
    split_x = table_x.reshape(table_x.shape[0], width_x, rows_x)
    split_y = table_y.reshape(table_y.shape[0], width_y, cols_y)
    part = jnp.einsum("cjy,bc->bjy", split_y, modes[0, 0], precision=FAST)
    part = jnp.einsum("bix,bjy->ijxy", split_x, part, precision=FAST)
    part = part.reshape(width_x * width_y, rows_x, cols_y)
    cells = lax.all_to_all(part, ("gx", "gy"), split_axis=0, concat_axis=0, tiled=True)
    return jnp.einsum("kz,kxy->zxy", table_z, cells, precision=FAST)[None]


def advance_terms(depth_index, depth, long_x, long_y):
    index_x = jnp.arange(long_x, dtype=jnp.int32).astype(jnp.float32)
    index_y = jnp.arange(long_y, dtype=jnp.int32).astype(jnp.float32)
    part_z = depth_index / depth * (depth_index / depth)
    part_x = index_x / long_x * (index_x / long_x)
    part_y = index_y / long_y * (index_y / long_y)
    theta = (
        COURANT
        * jnp.pi
        * jnp.sqrt(part_z[:, None, None] + part_x[None, :, None] + part_y[None, None, :])
    )
    shape = jnp.sinc(theta / (2.0 * jnp.pi))
    return 2.0 * jnp.cos(theta), COURANT * COURANT * shape * shape


def one_hot(index, count):
    return (index[:, None] == jnp.arange(count, dtype=jnp.int32)[None, :]).astype(jnp.float32)


def shards(modes_now, modes_old, pressure_now, source, strip_slot, strip_row):
    depth = source.shape[1]
    rows_x = source.shape[2]
    cols_y = source.shape[3]
    planes = modes_now.shape[1]
    long_x = modes_now.shape[2]
    long_y = modes_now.shape[3]
    block = lax.axis_index(("gx", "gy"))
    depth_index = (block * planes + jnp.arange(planes, dtype=jnp.int32)).astype(jnp.float32)
    table_z = lax.optimization_barrier(cosine_table(depth))
    table_x = lax.optimization_barrier(cosine_table(long_x))
    table_y = lax.optimization_barrier(cosine_table(long_y))
    scale_now, scale_spec = advance_terms(depth_index, depth, long_x, long_y)
    top = jnp.stack(
        [pressure_now[0, depth - 1], pressure_now[0, depth - 2], pressure_now[0, depth - 3]], axis=1
    ).reshape(rows_x, 3 * cols_y)
    bottom = jnp.transpose(pressure_now[0, 0:3], (1, 0, 2)).reshape(rows_x, 3 * cols_y)
    devices = lax.axis_size(("grp", "gx", "gy"))
    slots_per = max(2, rows_x // devices)
    total = devices * slots_per
    slots = strip_slot.reshape(-1)
    rows = strip_row.reshape(-1)
    label = jnp.broadcast_to((rows + 1).astype(jnp.float32)[:, None], (rows_x, cols_y))
    send = one_hot(slots, total)
    payload = jnp.concatenate([top, label], axis=1)
    buffer = jnp.einsum("sk,sf->kf", send, payload, precision=HIGH)
    got = lax.all_to_all(buffer, ("grp", "gx", "gy"), split_axis=0, concat_axis=0, tiled=True)
    rims = got[:, : 3 * cols_y]
    marks = jnp.round(got[:, 3 * cols_y]).astype(jnp.int32) - 1
    base = scale_now * modes_now[0] - modes_old[0]
    marks, base, scale_spec = lax.optimization_barrier((marks, base, scale_spec))
    live = (marks >= 0).astype(jnp.float32)[:, None]
    meet = one_hot(marks, rows_x)
    met = jnp.einsum("kr,rf->kf", meet, bottom, precision=HIGH)
    diff = met - rims
    first = diff[:, :cols_y]
    second = diff[:, cols_y : 2 * cols_y]
    third = diff[:, 2 * cols_y :]
    force = jnp.concatenate(
        [
            WEIGHTS[0] * first + WEIGHTS[1] * second + WEIGHTS[2] * third,
            WEIGHTS[1] * first + WEIGHTS[2] * second,
            WEIGHTS[2] * first,
        ],
        axis=1,
    ) * live
    back = lax.all_to_all(force, ("grp", "gx", "gy"), split_axis=0, concat_axis=0, tiled=True)
    top_force = jnp.einsum("sk,kf->sf", send, back, precision=HIGH).reshape(rows_x, 3, cols_y)
    bottom_force = jnp.einsum("kr,kf->rf", meet, -force, precision=HIGH).reshape(rows_x, 3, cols_y)
    forcing = source.at[:, 0:3].add(jnp.transpose(bottom_force, (1, 0, 2))[None])
    forcing = forcing.at[:, depth - 1].add(top_force[:, 0][None])
    forcing = forcing.at[:, depth - 2].add(top_force[:, 1][None])
    forcing = forcing.at[:, depth - 3].add(top_force[:, 2][None])
    spectrum = to_modes(forcing, table_z, table_x, table_y)
    modes_new = (base + scale_spec * spectrum[0])[None]
    pressure_next = to_cells(modes_new, table_z, table_x, table_y)
    return (modes_new, pressure_next)


def solution(mesh):
    placed = (
        P("grp", ("gx", "gy"), None, None),
        P("grp", ("gx", "gy"), None, None),
        P("grp", None, "gx", "gy"),
        P("grp", None, "gx", "gy"),
        P("grp", "gx", "gy"),
        P("grp", "gx", "gy"),
    )
    return jax.shard_map(
        shards,
        mesh=mesh,
        in_specs=placed,
        out_specs=(P("grp", ("gx", "gy"), None, None), P("grp", None, "gx", "gy")),
        check_vma=False,
    )
```

```python
import jax
import jax.numpy as jnp
from jax import lax
from jax.sharding import PartitionSpec as P

COURANT = 0.5
WEIGHTS = (1.5, -0.15, 2.0 / 180.0)
HIGH = lax.Precision.HIGHEST
FAST = lax.Precision.HIGH


def cosine_table(count):
    rows = jnp.arange(count, dtype=jnp.int32).astype(jnp.float32)[:, None]
    cols = jnp.arange(count, dtype=jnp.int32).astype(jnp.float32)[None, :]
    scale = jnp.where(rows == 0, jnp.sqrt(1.0 / count), jnp.sqrt(2.0 / count))
    return scale * jnp.cos(jnp.pi * rows * (cols + 0.5) / count)


def face_stencil(diff):
    first = diff[..., 0, :]
    second = diff[..., 1, :]
    third = diff[..., 2, :]
    return jnp.stack(
        [
            WEIGHTS[0] * first + WEIGHTS[1] * second + WEIGHTS[2] * third,
            WEIGHTS[1] * first + WEIGHTS[2] * second,
            WEIGHTS[2] * first,
        ],
        axis=-2,
    )


def gy_major(table_z, width_x, width_y):
    depth = table_z.shape[1]
    return table_z.reshape(width_x, width_y, depth).transpose(1, 0, 2).reshape(-1, depth)


def to_modes(field, table_z, table_x, table_y):
    width_x = lax.axis_size("gx")
    width_y = lax.axis_size("gy")
    rows_x = field.shape[2]
    cols_y = field.shape[3]
    table_p = gy_major(table_z, width_x, width_y)
    part = jnp.einsum("kz,zxy->kxy", table_p, field[0], precision=FAST)
    part = lax.all_to_all(part, ("gy", "gx"), split_axis=0, concat_axis=0, tiled=True)
    part = part.reshape(width_y, width_x, rows_x, cols_y)
    split_x = table_x.reshape(table_x.shape[0], width_x, rows_x)
    split_y = table_y.reshape(table_y.shape[0], width_y, cols_y)
    part = jnp.einsum("bix,jixy->bjy", split_x, part, precision=FAST)
    return jnp.einsum("cjy,bjy->bc", split_y, part, precision=FAST)[None, None]


def to_cells(modes, table_z, table_x, table_y):
    width_x = lax.axis_size("gx")
    width_y = lax.axis_size("gy")
    rows_x = modes.shape[2] // width_x
    cols_y = modes.shape[3] // width_y
    split_x = table_x.reshape(table_x.shape[0], width_x, rows_x)
    split_y = table_y.reshape(table_y.shape[0], width_y, cols_y)
    part = jnp.einsum("cjy,bc->bjy", split_y, modes[0, 0], precision=FAST)
    part = jnp.einsum("bix,bjy->jixy", split_x, part, precision=FAST)
    part = part.reshape(width_x * width_y, rows_x, cols_y)
    cells = lax.all_to_all(part, ("gy", "gx"), split_axis=0, concat_axis=0, tiled=True)
    table_p = gy_major(table_z, width_x, width_y)
    return jnp.einsum("kz,kxy->zxy", table_p, cells, precision=FAST)[None]


def advance_terms(depth_index, depth, long_x, long_y):
    index_x = jnp.arange(long_x, dtype=jnp.int32).astype(jnp.float32)
    index_y = jnp.arange(long_y, dtype=jnp.int32).astype(jnp.float32)
    part_z = depth_index / depth * (depth_index / depth)
    part_x = index_x / long_x * (index_x / long_x)
    part_y = index_y / long_y * (index_y / long_y)
    theta = (
        COURANT
        * jnp.pi
        * jnp.sqrt(part_z[:, None, None] + part_x[None, :, None] + part_y[None, None, :])
    )
    shape = jnp.sinc(theta / (2.0 * jnp.pi))
    return 2.0 * jnp.cos(theta), COURANT * COURANT * shape * shape


def one_hot(index, count):
    return (index[:, None] == jnp.arange(count, dtype=jnp.int32)[None, :]).astype(jnp.float32)


def shards(modes_now, modes_old, pressure_now, source, strip_slot, strip_row):
    depth = source.shape[1]
    rows_x = source.shape[2]
    cols_y = source.shape[3]
    planes = modes_now.shape[1]
    long_x = modes_now.shape[2]
    long_y = modes_now.shape[3]
    block = lax.axis_index(("gx", "gy"))
    depth_index = (block * planes + jnp.arange(planes, dtype=jnp.int32)).astype(jnp.float32)
    table_z = lax.optimization_barrier(cosine_table(depth))
    table_x = lax.optimization_barrier(cosine_table(long_x))
    table_y = lax.optimization_barrier(cosine_table(long_y))
    scale_now, scale_spec = advance_terms(depth_index, depth, long_x, long_y)
    scale_now = lax.optimization_barrier(scale_now)
    scale_spec = lax.optimization_barrier(scale_spec)
    top = jnp.stack(
        [pressure_now[0, depth - 1], pressure_now[0, depth - 2], pressure_now[0, depth - 3]], axis=1
    ).reshape(rows_x, 3 * cols_y)
    bottom = jnp.transpose(pressure_now[0, 0:3], (1, 0, 2)).reshape(rows_x, 3 * cols_y)
    devices = lax.axis_size(("grp", "gx", "gy"))
    slots_per = max(2, rows_x // devices)
    total = devices * slots_per
    slots = strip_slot.reshape(-1)
    rows = strip_row.reshape(-1)
    label = jnp.broadcast_to((rows + 1).astype(jnp.float32)[:, None], (rows_x, cols_y))
    send = one_hot(slots, total)
    payload = jnp.concatenate([top, label], axis=1)
    buffer = jnp.einsum("sk,sf->kf", send, payload, precision=HIGH)
    got = lax.all_to_all(buffer, ("grp", "gx", "gy"), split_axis=0, concat_axis=0, tiled=True)
    rims = got[:, : 3 * cols_y]
    marks = jnp.round(got[:, 3 * cols_y]).astype(jnp.int32) - 1
    marks, scale_now, scale_spec = lax.optimization_barrier((marks, scale_now, scale_spec))
    live = (marks >= 0).astype(jnp.float32)[:, None]
    meet = one_hot(marks, rows_x)
    met = jnp.einsum("kr,rf->kf", meet, bottom, precision=HIGH)
    diff = met - rims
    first = diff[:, :cols_y]
    second = diff[:, cols_y : 2 * cols_y]
    third = diff[:, 2 * cols_y :]
    force = jnp.concatenate(
        [
            WEIGHTS[0] * first + WEIGHTS[1] * second + WEIGHTS[2] * third,
            WEIGHTS[1] * first + WEIGHTS[2] * second,
            WEIGHTS[2] * first,
        ],
        axis=1,
    ) * live
    back = lax.all_to_all(force, ("grp", "gx", "gy"), split_axis=0, concat_axis=0, tiled=True)
    top_force = jnp.einsum("sk,kf->sf", send, back, precision=HIGH).reshape(rows_x, 3, cols_y)
    bottom_force = jnp.einsum("kr,kf->rf", meet, -force, precision=HIGH).reshape(rows_x, 3, cols_y)
    forcing = source.at[:, 0:3].add(jnp.transpose(bottom_force, (1, 0, 2))[None])
    forcing = forcing.at[:, depth - 1].add(top_force[:, 0][None])
    forcing = forcing.at[:, depth - 2].add(top_force[:, 1][None])
    forcing = forcing.at[:, depth - 3].add(top_force[:, 2][None])
    spectrum = to_modes(forcing, table_z, table_x, table_y)
    modes_new = (scale_now * modes_now[0] - modes_old[0] + scale_spec * spectrum[0])[None]
    pressure_next = to_cells(modes_new, table_z, table_x, table_y)
    return (modes_new, pressure_next)


def solution(mesh):
    placed = (
        P("grp", ("gx", "gy"), None, None),
        P("grp", ("gx", "gy"), None, None),
        P("grp", None, "gx", "gy"),
        P("grp", None, "gx", "gy"),
        P("grp", "gx", "gy"),
        P("grp", "gx", "gy"),
    )
    return jax.shard_map(
        shards,
        mesh=mesh,
        in_specs=placed,
        out_specs=(P("grp", ("gx", "gy"), None, None), P("grp", None, "gx", "gy")),
        check_vma=False,
    )
```

```python
import jax
import jax.numpy as jnp
from jax import lax
from jax.sharding import PartitionSpec as P

COURANT = 0.5
WEIGHTS = (1.5, -0.15, 2.0 / 180.0)
HIGH = lax.Precision.HIGHEST
FAST = lax.Precision.HIGH


def cosine_table(count):
    rows = jnp.arange(count, dtype=jnp.int32).astype(jnp.float32)[:, None]
    cols = jnp.arange(count, dtype=jnp.int32).astype(jnp.float32)[None, :]
    scale = jnp.where(rows == 0, jnp.sqrt(1.0 / count), jnp.sqrt(2.0 / count))
    return scale * jnp.cos(jnp.pi * rows * (cols + 0.5) / count)


def face_stencil(diff):
    first = diff[..., 0, :]
    second = diff[..., 1, :]
    third = diff[..., 2, :]
    return jnp.stack(
        [
            WEIGHTS[0] * first + WEIGHTS[1] * second + WEIGHTS[2] * third,
            WEIGHTS[1] * first + WEIGHTS[2] * second,
            WEIGHTS[2] * first,
        ],
        axis=-2,
    )


def gy_major(table_z, width_x, width_y):
    depth = table_z.shape[1]
    return table_z.reshape(width_x, width_y, depth).transpose(1, 0, 2).reshape(-1, depth)


def to_modes(field, table_z, table_x, table_y):
    width_x = lax.axis_size("gx")
    width_y = lax.axis_size("gy")
    rows_x = field.shape[2]
    cols_y = field.shape[3]
    table_p = gy_major(table_z, width_x, width_y)
    part = jnp.einsum("kz,zxy->kxy", table_p, field[0], precision=FAST)
    part = lax.all_to_all(part, ("gy", "gx"), split_axis=0, concat_axis=0, tiled=True)
    part = part.reshape(width_y, width_x, rows_x, cols_y)
    split_x = table_x.reshape(table_x.shape[0], width_x, rows_x)
    split_y = table_y.reshape(table_y.shape[0], width_y, cols_y)
    part = jnp.einsum("bix,jixy->bjy", split_x, part, precision=FAST)
    return jnp.einsum("cjy,bjy->bc", split_y, part, precision=FAST)[None, None]


def to_cells(modes, table_z, table_x, table_y):
    width_x = lax.axis_size("gx")
    width_y = lax.axis_size("gy")
    rows_x = modes.shape[2] // width_x
    cols_y = modes.shape[3] // width_y
    split_x = table_x.reshape(table_x.shape[0], width_x, rows_x)
    split_y = table_y.reshape(table_y.shape[0], width_y, cols_y)
    part = jnp.einsum("cjy,bc->bjy", split_y, modes[0, 0], precision=FAST)
    part = jnp.einsum("bix,bjy->jixy", split_x, part, precision=FAST)
    part = part.reshape(width_x * width_y, rows_x, cols_y)
    cells = lax.all_to_all(part, ("gy", "gx"), split_axis=0, concat_axis=0, tiled=True)
    table_p = gy_major(table_z, width_x, width_y)
    return jnp.einsum("kz,kxy->zxy", table_p, cells, precision=FAST)[None]


def advance_terms(depth_index, depth, long_x, long_y):
    index_x = jnp.arange(long_x, dtype=jnp.int32).astype(jnp.float32)
    index_y = jnp.arange(long_y, dtype=jnp.int32).astype(jnp.float32)
    part_z = depth_index / depth * (depth_index / depth)
    part_x = index_x / long_x * (index_x / long_x)
    part_y = index_y / long_y * (index_y / long_y)
    theta = (
        COURANT
        * jnp.pi
        * jnp.sqrt(part_z[:, None, None] + part_x[None, :, None] + part_y[None, None, :])
    )
    shape = jnp.sinc(theta / (2.0 * jnp.pi))
    return 2.0 * jnp.cos(theta), COURANT * COURANT * shape * shape


def one_hot(index, count):
    return (index[:, None] == jnp.arange(count, dtype=jnp.int32)[None, :]).astype(jnp.float32)


def shards(modes_now, modes_old, pressure_now, source, strip_slot, strip_row):
    depth = source.shape[1]
    rows_x = source.shape[2]
    cols_y = source.shape[3]
    planes = modes_now.shape[1]
    long_x = modes_now.shape[2]
    long_y = modes_now.shape[3]
    block = lax.axis_index(("gx", "gy"))
    depth_index = (block * planes + jnp.arange(planes, dtype=jnp.int32)).astype(jnp.float32)
    table_z = lax.optimization_barrier(cosine_table(depth))
    table_x = lax.optimization_barrier(cosine_table(long_x))
    table_y = lax.optimization_barrier(cosine_table(long_y))
    scale_now, scale_spec = advance_terms(depth_index, depth, long_x, long_y)
    scale_now = lax.optimization_barrier(scale_now)
    scale_spec = lax.optimization_barrier(scale_spec)
    upper = lax.optimization_barrier(lax.slice_in_dim(pressure_now[0], depth - 3, depth, axis=0))
    top = jnp.stack([upper[2], upper[1], upper[0]], axis=1).reshape(rows_x, 3 * cols_y)
    bottom = jnp.transpose(pressure_now[0, 0:3], (1, 0, 2)).reshape(rows_x, 3 * cols_y)
    devices = lax.axis_size(("grp", "gx", "gy"))
    slots_per = max(2, rows_x // devices)
    total = devices * slots_per
    slots = strip_slot.reshape(-1)
    rows = strip_row.reshape(-1)
    label = jnp.broadcast_to((rows + 1).astype(jnp.float32)[:, None], (rows_x, cols_y))
    send = one_hot(slots, total)
    payload = jnp.concatenate([top, label], axis=1)
    buffer = jnp.einsum("sk,sf->kf", send, payload, precision=HIGH)
    got = lax.all_to_all(buffer, ("grp", "gx", "gy"), split_axis=0, concat_axis=0, tiled=True)
    rims = got[:, : 3 * cols_y]
    marks = jnp.round(got[:, 3 * cols_y]).astype(jnp.int32) - 1
    marks, scale_now, scale_spec = lax.optimization_barrier((marks, scale_now, scale_spec))
    live = (marks >= 0).astype(jnp.float32)[:, None]
    meet = one_hot(marks, rows_x)
    met = jnp.einsum("kr,rf->kf", meet, bottom, precision=HIGH)
    diff = met - rims
    first = diff[:, :cols_y]
    second = diff[:, cols_y : 2 * cols_y]
    third = diff[:, 2 * cols_y :]
    force = jnp.concatenate(
        [
            WEIGHTS[0] * first + WEIGHTS[1] * second + WEIGHTS[2] * third,
            WEIGHTS[1] * first + WEIGHTS[2] * second,
            WEIGHTS[2] * first,
        ],
        axis=1,
    ) * live
    back = lax.all_to_all(force, ("grp", "gx", "gy"), split_axis=0, concat_axis=0, tiled=True)
    top_force = jnp.einsum("sk,kf->sf", send, back, precision=HIGH).reshape(rows_x, 3, cols_y)
    bottom_force = jnp.einsum("kr,kf->rf", meet, -force, precision=HIGH).reshape(rows_x, 3, cols_y)
    forcing = source.at[:, 0:3].add(jnp.transpose(bottom_force, (1, 0, 2))[None])
    forcing = forcing.at[:, depth - 1].add(top_force[:, 0][None])
    forcing = forcing.at[:, depth - 2].add(top_force[:, 1][None])
    forcing = forcing.at[:, depth - 3].add(top_force[:, 2][None])
    spectrum = to_modes(forcing, table_z, table_x, table_y)
    modes_new = (scale_now * modes_now[0] - modes_old[0] + scale_spec * spectrum[0])[None]
    pressure_next = to_cells(modes_new, table_z, table_x, table_y)
    return (modes_new, pressure_next)


def solution(mesh):
    placed = (
        P("grp", ("gx", "gy"), None, None),
        P("grp", ("gx", "gy"), None, None),
        P("grp", None, "gx", "gy"),
        P("grp", None, "gx", "gy"),
        P("grp", "gx", "gy"),
        P("grp", "gx", "gy"),
    )
    return jax.shard_map(
        shards,
        mesh=mesh,
        in_specs=placed,
        out_specs=(P("grp", ("gx", "gy"), None, None), P("grp", None, "gx", "gy")),
        check_vma=False,
    )
```

```python
import jax
import jax.numpy as jnp
from jax import lax
from jax.sharding import PartitionSpec as P

COURANT = 0.5
WEIGHTS = (1.5, -0.15, 2.0 / 180.0)
HIGH = lax.Precision.HIGHEST
FAST = lax.Precision.HIGH


def cosine_table(count):
    rows = jnp.arange(count, dtype=jnp.int32).astype(jnp.float32)[:, None]
    cols = jnp.arange(count, dtype=jnp.int32).astype(jnp.float32)[None, :]
    scale = jnp.where(rows == 0, jnp.sqrt(1.0 / count), jnp.sqrt(2.0 / count))
    return scale * jnp.cos(jnp.pi * rows * (cols + 0.5) / count)


def face_stencil(diff):
    first = diff[..., 0, :]
    second = diff[..., 1, :]
    third = diff[..., 2, :]
    return jnp.stack(
        [
            WEIGHTS[0] * first + WEIGHTS[1] * second + WEIGHTS[2] * third,
            WEIGHTS[1] * first + WEIGHTS[2] * second,
            WEIGHTS[2] * first,
        ],
        axis=-2,
    )


def gy_major(table_z, width_x, width_y):
    depth = table_z.shape[1]
    return table_z.reshape(width_x, width_y, depth).transpose(1, 0, 2).reshape(-1, depth)


def to_modes(field, table_z, table_x, table_y):
    width_x = lax.axis_size("gx")
    width_y = lax.axis_size("gy")
    rows_x = field.shape[2]
    cols_y = field.shape[3]
    table_p = gy_major(table_z, width_x, width_y)
    part = jnp.einsum("kz,zxy->kxy", table_p, field[0], precision=FAST)
    part = lax.all_to_all(part, ("gy", "gx"), split_axis=0, concat_axis=0, tiled=True)
    part = part.reshape(width_y, width_x, rows_x, cols_y)
    split_x = table_x.reshape(table_x.shape[0], width_x, rows_x)
    split_y = table_y.reshape(table_y.shape[0], width_y, cols_y)
    part = jnp.einsum("bix,jixy->bjy", split_x, part, precision=FAST)
    return jnp.einsum("cjy,bjy->bc", split_y, part, precision=FAST)[None, None]


def to_cells(modes, table_z, table_x, table_y):
    width_x = lax.axis_size("gx")
    width_y = lax.axis_size("gy")
    rows_x = modes.shape[2] // width_x
    cols_y = modes.shape[3] // width_y
    split_x = table_x.reshape(table_x.shape[0], width_x, rows_x)
    split_y = table_y.reshape(table_y.shape[0], width_y, cols_y)
    part = jnp.einsum("cjy,bc->bjy", split_y, modes[0, 0], precision=FAST)
    part = jnp.einsum("bix,bjy->jixy", split_x, part, precision=FAST)
    part = part.reshape(width_x * width_y, rows_x, cols_y)
    cells = lax.all_to_all(part, ("gy", "gx"), split_axis=0, concat_axis=0, tiled=True)
    table_p = gy_major(table_z, width_x, width_y)
    return jnp.einsum("kz,kxy->zxy", table_p, cells, precision=FAST)[None]


def advance_terms(depth_index, depth, long_x, long_y):
    index_x = jnp.arange(long_x, dtype=jnp.int32).astype(jnp.float32)
    index_y = jnp.arange(long_y, dtype=jnp.int32).astype(jnp.float32)
    part_z = depth_index / depth * (depth_index / depth)
    part_x = index_x / long_x * (index_x / long_x)
    part_y = index_y / long_y * (index_y / long_y)
    theta = (
        COURANT
        * jnp.pi
        * jnp.sqrt(part_z[:, None, None] + part_x[None, :, None] + part_y[None, None, :])
    )
    turns = theta / (2.0 * jnp.pi)
    shape = jnp.sinc(turns)
    half_sine = jnp.pi * turns * shape
    return 2.0 * (1.0 - 2.0 * half_sine * half_sine), COURANT * COURANT * shape * shape


def one_hot(index, count):
    return (index[:, None] == jnp.arange(count, dtype=jnp.int32)[None, :]).astype(jnp.float32)


def shards(modes_now, modes_old, pressure_now, source, strip_slot, strip_row):
    depth = source.shape[1]
    rows_x = source.shape[2]
    cols_y = source.shape[3]
    planes = modes_now.shape[1]
    long_x = modes_now.shape[2]
    long_y = modes_now.shape[3]
    block = lax.axis_index(("gx", "gy"))
    depth_index = (block * planes + jnp.arange(planes, dtype=jnp.int32)).astype(jnp.float32)
    table_z = lax.optimization_barrier(cosine_table(depth))
    table_x = lax.optimization_barrier(cosine_table(long_x))
    table_y = lax.optimization_barrier(cosine_table(long_y))
    scale_now, scale_spec = advance_terms(depth_index, depth, long_x, long_y)
    scale_now = lax.optimization_barrier(scale_now)
    scale_spec = lax.optimization_barrier(scale_spec)
    upper = lax.optimization_barrier(lax.slice_in_dim(pressure_now[0], depth - 3, depth, axis=0))
    top = jnp.stack([upper[2], upper[1], upper[0]], axis=1).reshape(rows_x, 3 * cols_y)
    bottom = jnp.transpose(pressure_now[0, 0:3], (1, 0, 2)).reshape(rows_x, 3 * cols_y)
    devices = lax.axis_size(("grp", "gx", "gy"))
    slots_per = max(2, rows_x // devices)
    total = devices * slots_per
    slots = strip_slot.reshape(-1)
    rows = strip_row.reshape(-1)
    label = jnp.broadcast_to((rows + 1).astype(jnp.float32)[:, None], (rows_x, cols_y))
    send = one_hot(slots, total)
    payload = jnp.concatenate([top, label], axis=1)
    buffer = jnp.einsum("sk,sf->kf", send, payload, precision=HIGH)
    got = lax.all_to_all(buffer, ("grp", "gx", "gy"), split_axis=0, concat_axis=0, tiled=True)
    rims = got[:, : 3 * cols_y]
    marks = jnp.round(got[:, 3 * cols_y]).astype(jnp.int32) - 1
    marks, scale_now, scale_spec = lax.optimization_barrier((marks, scale_now, scale_spec))
    live = (marks >= 0).astype(jnp.float32)[:, None]
    meet = one_hot(marks, rows_x)
    met = jnp.einsum("kr,rf->kf", meet, bottom, precision=HIGH)
    diff = met - rims
    first = diff[:, :cols_y]
    second = diff[:, cols_y : 2 * cols_y]
    third = diff[:, 2 * cols_y :]
    force = jnp.concatenate(
        [
            WEIGHTS[0] * first + WEIGHTS[1] * second + WEIGHTS[2] * third,
            WEIGHTS[1] * first + WEIGHTS[2] * second,
            WEIGHTS[2] * first,
        ],
        axis=1,
    ) * live
    back = lax.all_to_all(force, ("grp", "gx", "gy"), split_axis=0, concat_axis=0, tiled=True)
    top_force = jnp.einsum("sk,kf->sf", send, back, precision=HIGH).reshape(rows_x, 3, cols_y)
    bottom_force = jnp.einsum("kr,kf->rf", meet, -force, precision=HIGH).reshape(rows_x, 3, cols_y)
    forcing = source.at[:, 0:3].add(jnp.transpose(bottom_force, (1, 0, 2))[None])
    forcing = forcing.at[:, depth - 1].add(top_force[:, 0][None])
    forcing = forcing.at[:, depth - 2].add(top_force[:, 1][None])
    forcing = forcing.at[:, depth - 3].add(top_force[:, 2][None])
    spectrum = to_modes(forcing, table_z, table_x, table_y)
    modes_new = (scale_now * modes_now[0] - modes_old[0] + scale_spec * spectrum[0])[None]
    pressure_next = to_cells(modes_new, table_z, table_x, table_y)
    return (modes_new, pressure_next)


def solution(mesh):
    placed = (
        P("grp", ("gx", "gy"), None, None),
        P("grp", ("gx", "gy"), None, None),
        P("grp", None, "gx", "gy"),
        P("grp", None, "gx", "gy"),
        P("grp", "gx", "gy"),
        P("grp", "gx", "gy"),
    )
    return jax.shard_map(
        shards,
        mesh=mesh,
        in_specs=placed,
        out_specs=(P("grp", ("gx", "gy"), None, None), P("grp", None, "gx", "gy")),
        check_vma=False,
    )
```

```python
import jax
import jax.numpy as jnp
from jax import lax
from jax.sharding import PartitionSpec as P

COURANT = 0.5
WEIGHTS = (1.5, -0.15, 2.0 / 180.0)
HIGH = lax.Precision.HIGHEST
FAST = lax.Precision.HIGH


def cosine_table(count):
    rows = jnp.arange(count, dtype=jnp.int32).astype(jnp.float32)[:, None]
    cols = jnp.arange(count, dtype=jnp.int32).astype(jnp.float32)[None, :]
    scale = jnp.where(rows == 0, jnp.sqrt(1.0 / count), jnp.sqrt(2.0 / count))
    return scale * jnp.cos(jnp.pi * rows * (cols + 0.5) / count)


def face_stencil(diff):
    first = diff[..., 0, :]
    second = diff[..., 1, :]
    third = diff[..., 2, :]
    return jnp.stack(
        [
            WEIGHTS[0] * first + WEIGHTS[1] * second + WEIGHTS[2] * third,
            WEIGHTS[1] * first + WEIGHTS[2] * second,
            WEIGHTS[2] * first,
        ],
        axis=-2,
    )


def gy_major(table_z, width_x, width_y):
    depth = table_z.shape[1]
    return table_z.reshape(width_x, width_y, depth).transpose(1, 0, 2).reshape(-1, depth)


def to_modes(field, table_z, table_x, table_y):
    width_x = lax.axis_size("gx")
    width_y = lax.axis_size("gy")
    rows_x = field.shape[2]
    cols_y = field.shape[3]
    table_p = gy_major(table_z, width_x, width_y)
    part = jnp.einsum("kz,zxy->kxy", table_p, field[0], precision=FAST)
    part = lax.all_to_all(part, ("gy", "gx"), split_axis=0, concat_axis=0, tiled=True)
    part = part.reshape(width_y, width_x, rows_x, cols_y)
    split_x = table_x.reshape(table_x.shape[0], width_x, rows_x)
    split_y = table_y.reshape(table_y.shape[0], width_y, cols_y)
    part = jnp.einsum("bix,jixy->bjy", split_x, part, precision=FAST)
    return jnp.einsum("cjy,bjy->bc", split_y, part, precision=FAST)[None, None]


def to_cells(modes, table_z, table_x, table_y):
    width_x = lax.axis_size("gx")
    width_y = lax.axis_size("gy")
    rows_x = modes.shape[2] // width_x
    cols_y = modes.shape[3] // width_y
    split_x = table_x.reshape(table_x.shape[0], width_x, rows_x)
    split_y = table_y.reshape(table_y.shape[0], width_y, cols_y)
    part = jnp.einsum("cjy,bc->bjy", split_y, modes[0, 0], precision=FAST)
    part = jnp.einsum("bix,bjy->jixy", split_x, part, precision=FAST)
    part = part.reshape(width_x * width_y, rows_x, cols_y)
    cells = lax.all_to_all(part, ("gy", "gx"), split_axis=0, concat_axis=0, tiled=True)
    table_p = gy_major(table_z, width_x, width_y)
    return jnp.einsum("kz,kxy->zxy", table_p, cells, precision=FAST)[None]


def advance_terms(depth_index, depth, long_x, long_y):
    index_x = jnp.arange(long_x, dtype=jnp.int32).astype(jnp.float32)
    index_y = jnp.arange(long_y, dtype=jnp.int32).astype(jnp.float32)
    part_z = depth_index / depth * (depth_index / depth)
    part_x = index_x / long_x * (index_x / long_x)
    part_y = index_y / long_y * (index_y / long_y)
    theta = (
        COURANT
        * jnp.pi
        * jnp.sqrt(part_z[:, None, None] + part_x[None, :, None] + part_y[None, None, :])
    )
    turns = theta / (2.0 * jnp.pi)
    shape = jnp.sinc(turns)
    half_sine = jnp.pi * turns * shape
    return 2.0 * (1.0 - 2.0 * half_sine * half_sine), COURANT * COURANT * shape * shape


def one_hot(index, count):
    return (index[:, None] == jnp.arange(count, dtype=jnp.int32)[None, :]).astype(jnp.float32)


def shards(modes_now, modes_old, pressure_now, source, strip_slot, strip_row):
    depth = source.shape[1]
    rows_x = source.shape[2]
    cols_y = source.shape[3]
    planes = modes_now.shape[1]
    long_x = modes_now.shape[2]
    long_y = modes_now.shape[3]
    block = lax.axis_index(("gx", "gy"))
    depth_index = (block * planes + jnp.arange(planes, dtype=jnp.int32)).astype(jnp.float32)
    table_z = lax.optimization_barrier(cosine_table(depth))
    table_x = lax.optimization_barrier(cosine_table(long_x))
    table_y = lax.optimization_barrier(cosine_table(long_y))
    scale_now, scale_spec = advance_terms(depth_index, depth, long_x, long_y)
    scale_now = lax.optimization_barrier(scale_now)
    scale_spec = lax.optimization_barrier(scale_spec)
    upper = lax.optimization_barrier(lax.slice_in_dim(pressure_now[0], depth - 3, depth, axis=0))
    top = jnp.stack([upper[2], upper[1], upper[0]], axis=1).reshape(rows_x, 3 * cols_y)
    bottom = jnp.transpose(pressure_now[0, 0:3], (1, 0, 2)).reshape(rows_x, 3 * cols_y)
    devices = lax.axis_size(("grp", "gx", "gy"))
    slots_per = max(2, rows_x // devices)
    total = devices * slots_per
    slots = strip_slot.reshape(-1)
    rows = strip_row.reshape(-1)
    label = jnp.broadcast_to((rows + 1).astype(jnp.float32)[:, None], (rows_x, cols_y))
    send = one_hot(slots, total)
    payload = jnp.concatenate([top, label], axis=1)
    buffer = jnp.einsum("sk,sf->kf", send, payload, precision=HIGH)
    got = lax.all_to_all(buffer, ("grp", "gx", "gy"), split_axis=0, concat_axis=0, tiled=True)
    rims = got[:, : 3 * cols_y]
    marks = jnp.round(got[:, 3 * cols_y]).astype(jnp.int32) - 1
    marks, scale_now, scale_spec = lax.optimization_barrier((marks, scale_now, scale_spec))
    live = (marks >= 0).astype(jnp.float32)[:, None]
    meet = one_hot(marks, rows_x)
    met = jnp.einsum("kr,rf->kf", meet, bottom, precision=HIGH)
    diff = met - rims
    first = diff[:, :cols_y]
    second = diff[:, cols_y : 2 * cols_y]
    third = diff[:, 2 * cols_y :]
    force = jnp.concatenate(
        [
            WEIGHTS[0] * first + WEIGHTS[1] * second + WEIGHTS[2] * third,
            WEIGHTS[1] * first + WEIGHTS[2] * second,
            WEIGHTS[2] * first,
        ],
        axis=1,
    ) * live
    back = lax.all_to_all(force, ("grp", "gx", "gy"), split_axis=0, concat_axis=0, tiled=True)
    top_force = jnp.einsum("sk,kf->sf", send, back, precision=HIGH).reshape(rows_x, 3, cols_y)
    bottom_force = jnp.einsum("kr,kf->rf", meet, -force, precision=HIGH).reshape(rows_x, 3, cols_y)
    upper_force = jnp.stack([top_force[:, 2], top_force[:, 1], top_force[:, 0]], axis=0)
    forcing = jnp.concatenate(
        [
            source[0, 0:3] + jnp.transpose(bottom_force, (1, 0, 2)),
            source[0, 3 : depth - 3],
            source[0, depth - 3 :] + upper_force,
        ],
        axis=0,
    )[None]
    spectrum = to_modes(forcing, table_z, table_x, table_y)
    modes_new = (scale_now * modes_now[0] - modes_old[0] + scale_spec * spectrum[0])[None]
    pressure_next = to_cells(modes_new, table_z, table_x, table_y)
    return (modes_new, pressure_next)


def solution(mesh):
    placed = (
        P("grp", ("gx", "gy"), None, None),
        P("grp", ("gx", "gy"), None, None),
        P("grp", None, "gx", "gy"),
        P("grp", None, "gx", "gy"),
        P("grp", "gx", "gy"),
        P("grp", "gx", "gy"),
    )
    return jax.shard_map(
        shards,
        mesh=mesh,
        in_specs=placed,
        out_specs=(P("grp", ("gx", "gy"), None, None), P("grp", None, "gx", "gy")),
        check_vma=False,
    )
```
